256 devices in a mesh: seq: 32 (over y, z), ch: 8 (over x, core).
Axes of the slice: x: 4, y: 4, z: 8, core: 2. Of those that a mesh axis runs over, the one named last changes fastest.
Arguments:
- hidden_in: bfloat16 [65536, 2048], P('seq', 'ch'), may hold values from -6 to 6
- grad_out: bfloat16 [65536, 2048], P('seq', 'ch'), may hold values from -6 to 6
- norm_gain: bfloat16 [2048], P('ch'), may hold values from 0.099609375 to 1.8984375
- skip_weight: float32 [2048], P('ch'), may hold values from -4 to 4
- filter_coef: bfloat16 [64, 2, 2048], P(None, None, 'ch'), may hold values from -0.75 to 0.75
- run_lengths: int32 [64], replicated, may hold values from 1 to 4096, 65536 in all
Outputs:
- hidden_grad: bfloat16 [65536, 2048], P('seq', 'ch')
- filter_grad: float32 [64, 2, 2048], P('seq', None, 'ch')
The draws below stay inside these ranges and needn't reach their ends.
Inputs may be any that keep to these rules, and one draw needn't show every extreme that they name: `run_lengths`: runs lie end to end from token 0, documents at even positions and padding at odd ones; they sum to 65536, and the longest has exactly 4096 tokens.
All inputs are finite; a program needn't handle non-finite values.
Results may differ from the reference program's by a relative error of at most 0.0095.
Values may be sent and summed in bfloat16 or wider, within the bound.
No kernel may reach another device: no remote copies, remote signals or barrier semaphores. Data moves between devices by JAX's collectives and lax.ppermute only.
A program may use at most 64 MiB of HBM per device.

```python
import math
import jax
import jax.numpy as jnp
import numpy as np
from jax import lax

D = 2048
BLOCK = 512
FEAT = 64
RUNS = 64
SEQ_LEN = 65536
N_CH = 8


def block_scale(stream_key, extent, shards, low, high):
    level, own = 1.0, jax.random.fold_in(stream_key, 6)
    for axis_at, shards_of in shards:
        steps = jnp.exp(jax.random.uniform(jax.random.fold_in(own, axis_at), (shards_of,), jnp.float32, low / len(shards), high / len(shards)))
        level = level * jnp.repeat(steps, extent[axis_at] // shards_of).reshape([-1 if axis == axis_at else 1 for axis in range(len(extent))])
    return level


def split_up(amount, total, most, slope):
    weights = [(1 << 20) // math.isqrt(grade ** slope) + 1 for grade in range(2, amount + 1)]
    spare, given = total - most - (amount - 1), [1] * (amount - 1)
    while spare > 0:
        free = [i for i in range(amount - 1) if given[i] < most]
        pool, remaining = sum([weights[i] for i in free]), spare
        for i in free:
            extra = min(most - given[i], max(1, remaining * weights[i] // pool), spare)
            given[i] = given[i] + extra
            spare = spare - extra
    return np.array([most] + given)


def uneven_parts(own_key, number_of, total, most, skew):
    if number_of == 2:
        one = jax.random.randint(own_key, (), max(1, total - most), min(most, total - 1) + 1)
        return jnp.stack([one, total - one])
    sizes = jnp.asarray(split_up(number_of, total, most, skew), jnp.int32)
    pairs = (number_of - 1) // 2
    giver, sink = sizes[1:1 + 2 * pairs:2], sizes[2:2 + 2 * pairs:2]
    margin = jnp.minimum(giver - 1, most - sink)
    moved = jax.random.randint(jax.random.fold_in(own_key, 1), (pairs,), 0, 1 << 20) % (margin + 1)
    sizes = sizes.at[1:1 + 2 * pairs:2].set(giver - moved).at[2:2 + 2 * pairs:2].set(sink + moved)
    return sizes[jax.random.permutation(jax.random.fold_in(own_key, 2), number_of)]


def centred(rng, extent, scale, limit, pieces=(), held_as=jnp.bfloat16):
    loudness = block_scale(rng, extent, pieces, -0.22, 0.18) if pieces else 1.0
    entries = jax.random.normal(rng, extent, jnp.float32) * scale * loudness
    return jnp.minimum(jnp.maximum(entries, -limit), limit).astype(held_as)


def setup_inputs(seed: int = 0) -> dict:
    keys = jax.random.split(jax.random.key(seed), 7)
    hidden_in = centred(keys[0], (SEQ_LEN, D), 1.0, 6.0, ((0, 32), (1, 8)))
    grad_out = centred(keys[1], (SEQ_LEN, D), 1.0, 6.0, ((0, 32), (1, 8)))
    norm_gain = jnp.clip(1.0 + 0.18 * jax.random.normal(keys[2], (D,), jnp.float32), 0.099609375, 1.8984375).astype(jnp.bfloat16)
    skip_weight = centred(keys[3], (D,), 1.0, 4.0, ((0, 8),), jnp.float32)
    filter_coef = centred(keys[4], (FEAT, 2, D), FEAT ** -0.5, 0.75, ((2, 8),))
    run_lengths = uneven_parts(keys[5], RUNS, SEQ_LEN, 4 * SEQ_LEN // RUNS, 2).astype(jnp.int32)
    return dict(hidden_in=hidden_in, grad_out=grad_out, norm_gain=norm_gain, skip_weight=skip_weight, filter_coef=filter_coef, run_lengths=run_lengths)


epsilon = 1e-06

def halved(value):
    return lax.optimization_barrier(value.astype(jnp.bfloat16)).astype(jnp.float32)

def twin_table(count, sign):
    indices = jnp.arange(count, dtype=jnp.int32)
    product = indices[:, None] * indices[None, :] % count
    angles = 2.0 * math.pi / count * product.astype(jnp.float32)
    factor = 1.0 / math.sqrt(count)
    return (jnp.cos(angles) * factor, sign * jnp.sin(angles) * factor)

def block_matrix(count, sign):
    cosine, sine_part = twin_table(count, sign)
    upper = jnp.concatenate([cosine, sine_part], axis=1)
    lower = jnp.concatenate([-sine_part, cosine], axis=1)
    return jnp.concatenate([upper, lower], axis=0)

def twist(parts, freq_index, pos_index, seq_total, sign):
    product = (freq_index[:, None] * pos_index[None, :]).astype(jnp.float32)
    angles = 2.0 * math.pi / seq_total * product
    cosine = jnp.cos(angles)[:, :, None]
    sine_part = (sign * jnp.sin(angles))[:, :, None]
    real_part = parts[:, 0] * cosine - parts[:, 1] * sine_part
    imag_part = parts[:, 0] * sine_part + parts[:, 1] * cosine
    return jnp.stack([real_part, imag_part], axis=1)

def features(freq_index, seq_total):
    orders = 2 * jnp.arange(FEAT, dtype=jnp.int32) + 1
    product = freq_index[..., None] * orders % seq_total
    return jnp.cos(2.0 * math.pi / seq_total * product.astype(jnp.float32))

def reference(hidden_in, grad_out, norm_gain, skip_weight, filter_coef, run_lengths):
    seq_total = hidden_in.shape[0]
    nblocks = seq_total // BLOCK
    groups = N_CH
    group_width = D // groups
    upcast = hidden_in.astype(jnp.float32)
    inverse_rms = lax.rsqrt(lax.optimization_barrier(jnp.sum(upcast * upcast, axis=1)) / D + epsilon)
    gain = norm_gain.astype(jnp.float32)
    normed = (upcast * inverse_rms[:, None] * gain[None, :]).astype(jnp.bfloat16)
    run_ends = jnp.cumsum(run_lengths).astype(jnp.int32)
    positions = jnp.arange(seq_total, dtype=jnp.int32)
    run_index = lax.optimization_barrier(jnp.sum((run_ends[None, :] <= positions[:, None]).astype(jnp.int32), axis=1))
    keep = run_index % 2 == 0
    gated = jnp.where(keep[:, None], grad_out, jnp.zeros_like(grad_out))
    block_ids = jnp.arange(nblocks, dtype=jnp.int32)
    inner_ids = jnp.arange(BLOCK, dtype=jnp.int32)
    freq_grid = inner_ids[None, :] * nblocks + block_ids[:, None]
    feat_table = halved(features(freq_grid, seq_total))
    forward_first = halved(jnp.stack(twin_table(nblocks, -1.0), axis=2))
    forward_second = halved(block_matrix(BLOCK, -1.0))
    back_first = halved(block_matrix(BLOCK, 1.0))
    cosine, sine_part = twin_table(nblocks, 1.0)
    back_second = halved(jnp.stack([cosine, -sine_part], axis=1))

    def to_freq(field):
        blocks = field.astype(jnp.float32).reshape(nblocks, BLOCK, -1)
        parts = jnp.einsum('nmc,nkr->krmc', blocks, forward_first)
        turned = halved(twist(parts, block_ids, inner_ids, seq_total, -1.0))
        flat = turned.reshape(nblocks, 2 * BLOCK, -1)
        return jnp.einsum('kmc,mj->kjc', flat, forward_second).reshape(nblocks, 2, BLOCK, -1)

    def to_time(spectrum):
        flat = spectrum.astype(jnp.float32).reshape(nblocks, 2 * BLOCK, -1)
        parts = jnp.einsum('kmc,mj->kjc', flat, back_first).reshape(nblocks, 2, BLOCK, -1)
        turned = halved(twist(parts, block_ids, inner_ids, seq_total, 1.0))
        return jnp.einsum('krmc,krn->nmc', turned, back_second).reshape(seq_total, -1)

    def group_pass(operands):
        normed_part, gated_part, coef_part, skip_part = operands
        spec_normed = to_freq(normed_part)
        spec_gated = to_freq(gated_part)
        response = jnp.einsum('kbj,jrc->krbc', feat_table, coef_part.astype(jnp.float32))
        grad_real = spec_normed[:, 0] * spec_gated[:, 0] + spec_normed[:, 1] * spec_gated[:, 1]
        grad_imag = spec_normed[:, 0] * spec_gated[:, 1] - spec_normed[:, 1] * spec_gated[:, 0]
        spec_grad = jnp.stack([grad_real, grad_imag], axis=1).astype(jnp.bfloat16)
        coef_grad = jnp.einsum('kbj,krbc->jrc', feat_table, spec_grad.astype(jnp.float32)) / math.sqrt(seq_total)
        prod_real = response[:, 0] * spec_gated[:, 0] + response[:, 1] * spec_gated[:, 1]
        prod_imag = response[:, 0] * spec_gated[:, 1] - response[:, 1] * spec_gated[:, 0]
        product = jnp.stack([prod_real, prod_imag], axis=1).astype(jnp.bfloat16)
        conv_grad = to_time(product)
        normed_grad = conv_grad + skip_part[None, :] * gated_part.astype(jnp.float32)
        return (normed_grad, coef_grad)
    normed_groups = normed.reshape(seq_total, groups, group_width).transpose(1, 0, 2)
    gated_groups = gated.reshape(seq_total, groups, group_width).transpose(1, 0, 2)
    coef_groups = filter_coef.reshape(FEAT, 2, groups, group_width).transpose(2, 0, 1, 3)
    skip_groups = skip_weight.reshape(groups, group_width)
    grad_groups, coef_grads = lax.map(group_pass, (normed_groups, gated_groups, coef_groups, skip_groups))
    normed_grad = grad_groups.transpose(1, 0, 2).reshape(seq_total, D)
    filter_grad = coef_grads.transpose(1, 2, 0, 3).reshape(FEAT, 2, D)
    scaled_grad = gain[None, :] * normed_grad
    row_dot = lax.optimization_barrier(jnp.sum(scaled_grad * upcast, axis=1))
    hidden_grad = inverse_rms[:, None] * scaled_grad - upcast * (inverse_rms ** 3 * row_dot / D)[:, None]
    return (hidden_grad.astype(jnp.bfloat16), filter_grad)
```

```python
import math

import jax
import jax.numpy as jnp
from jax import lax
from jax.sharding import PartitionSpec as P

D = 2048
BLOCK = 512
FEAT = 64


epsilon = 1e-06


def from_everyone(value, axis):
    copies = jnp.broadcast_to(value, (lax.axis_size(axis), *value.shape))
    return lax.all_to_all(copies, axis, split_axis=0, concat_axis=0, tiled=True)


def taken_together(value, axis):
    return lax.psum(value, axis)


def twin_table(count, sign):
    indices = jnp.arange(count, dtype=jnp.int32)
    product = indices[:, None] * indices[None, :] % count
    angles = 2.0 * math.pi / count * product.astype(jnp.float32)
    factor = 1.0 / math.sqrt(count)
    return (jnp.cos(angles) * factor, sign * jnp.sin(angles) * factor)


def block_matrix(count, sign):
    cosine, sine_part = twin_table(count, sign)
    upper = jnp.concatenate([cosine, sine_part], axis=1)
    lower = jnp.concatenate([-sine_part, cosine], axis=1)
    return jnp.concatenate([upper, lower], axis=0)


def twist_leading(parts, freq_index, pos_index, seq_total, sign):
    product = (freq_index[:, None] * pos_index[None, :]).astype(jnp.float32)
    angles = 2.0 * math.pi / seq_total * product
    cosine = jnp.cos(angles)[None, :, :]
    sine_part = (sign * jnp.sin(angles))[None, :, :]
    real_part = parts[:, :, 0] * cosine - parts[:, :, 1] * sine_part
    imag_part = parts[:, :, 0] * sine_part + parts[:, :, 1] * cosine
    return jnp.stack([real_part, imag_part], axis=2)


def features(freq_index, seq_total):
    orders = 2 * jnp.arange(FEAT, dtype=jnp.int32) + 1
    product = freq_index[..., None] * orders % seq_total
    return jnp.cos(2.0 * math.pi / seq_total * product.astype(jnp.float32))


def feature_factors(inner, nblocks, seq_total):
    orders = 2 * jnp.arange(FEAT, dtype=jnp.int32) + 1
    inner_ids = jnp.arange(inner, dtype=jnp.int32)
    block_ids = jnp.arange(nblocks, dtype=jnp.int32)
    inner_prod = (inner_ids[:, None] * orders[None, :]) % inner
    block_prod = (block_ids[:, None] * orders[None, :]) % seq_total
    inner_ang = 2.0 * math.pi / inner * inner_prod.astype(jnp.float32)
    block_ang = 2.0 * math.pi / seq_total * block_prod.astype(jnp.float32)
    inner_tab = jnp.concatenate([jnp.cos(inner_ang), jnp.sin(inner_ang)], axis=1)
    return inner_tab, jnp.cos(block_ang), jnp.sin(block_ang)


def per_device(hidden_in, grad_out, norm_gain, skip_weight, filter_coef, run_lengths):
    local_tokens = hidden_in.shape[0]
    local_width = hidden_in.shape[1]
    seq_parts = lax.axis_size("seq")
    seq_rank = lax.axis_index("seq")
    seq_total = local_tokens * seq_parts
    nblocks = seq_total // BLOCK
    upcast = hidden_in.astype(jnp.float32)
    square_sums = taken_together(jnp.sum(upcast * upcast, axis=1), "ch")
    inverse_rms = lax.rsqrt(square_sums / D + epsilon)
    gain = norm_gain.astype(jnp.float32)
    normed = (upcast * inverse_rms[:, None] * gain[None, :]).astype(jnp.bfloat16)
    run_ends = jnp.cumsum(run_lengths)
    positions = seq_rank * local_tokens + jnp.arange(local_tokens, dtype=jnp.int32)
    run_index = jnp.sum((run_ends[None, :] <= positions[:, None]).astype(jnp.int32), axis=1)
    keep = run_index % 2 == 0
    gated = jnp.where(keep[:, None], grad_out, jnp.zeros_like(grad_out))
    forward_first = jnp.stack(twin_table(nblocks, -1.0), axis=2).astype(jnp.bfloat16)
    forward_second = block_matrix(BLOCK, -1.0).astype(jnp.bfloat16)
    back_first = block_matrix(BLOCK, 1.0).astype(jnp.bfloat16)
    cosine, sine_part = twin_table(nblocks, 1.0)
    back_second = jnp.stack([cosine, -sine_part], axis=1).astype(jnp.bfloat16)
    block_ids = jnp.arange(nblocks, dtype=jnp.int32)
    all_inner = jnp.arange(BLOCK, dtype=jnp.int32)
    width_share = local_width // seq_parts
    normed, gated = lax.optimization_barrier((normed, gated))
    moved = (
        lax.all_to_all(normed.T, "seq", split_axis=0, concat_axis=1, tiled=True),
        lax.all_to_all(gated.T, "seq", split_axis=0, concat_axis=1, tiled=True),
    )
    coef_part = lax.dynamic_slice_in_dim(filter_coef, seq_rank * width_share, width_share, 2)

    def local_freq(field):
        blocks = field.reshape(width_share, nblocks, BLOCK)
        parts = jnp.einsum(
            "cnm,nkr->ckrm", blocks, forward_first, preferred_element_type=jnp.float32
        )
        turned = twist_leading(parts, block_ids, all_inner, seq_total, -1.0).astype(jnp.bfloat16)
        flat = turned.reshape(width_share, nblocks, 2 * BLOCK)
        spectrum = jnp.einsum(
            "ckm,mj->ckj", flat, forward_second, preferred_element_type=jnp.float32
        )
        return spectrum.reshape(width_share, nblocks, 2, BLOCK)

    spec_normed = local_freq(moved[0])
    spec_gated = local_freq(moved[1])
    inner_tab, block_cos, block_sin = feature_factors(BLOCK, nblocks, seq_total)
    coef_t = coef_part.astype(jnp.float32).transpose(2, 1, 0)[:, None, :, :]
    coef_mix = jnp.concatenate(
        [block_cos[None, :, None, :] * coef_t, -block_sin[None, :, None, :] * coef_t], axis=3
    )
    response = jnp.einsum(
        "ckrj,bj->ckrb", coef_mix, inner_tab,
        precision=lax.Precision.HIGHEST, preferred_element_type=jnp.float32,
    )
    grad_real = (
        spec_normed[:, :, 0] * spec_gated[:, :, 0] + spec_normed[:, :, 1] * spec_gated[:, :, 1]
    )
    grad_imag = (
        spec_normed[:, :, 0] * spec_gated[:, :, 1] - spec_normed[:, :, 1] * spec_gated[:, :, 0]
    )
    spec_grad = jnp.stack([grad_real, grad_imag], axis=2).astype(jnp.bfloat16)
    partial = jnp.einsum(
        "ckrb,bj->ckrj", spec_grad.astype(jnp.float32), inner_tab,
        precision=lax.Precision.HIGHEST, preferred_element_type=jnp.float32,
    )
    coef_local = jnp.einsum(
        "ckrj,kj->jrc", partial[..., :FEAT], block_cos, precision=lax.Precision.HIGHEST
    ) - jnp.einsum(
        "ckrj,kj->jrc", partial[..., FEAT:], block_sin, precision=lax.Precision.HIGHEST
    )
    coef_sum = lax.all_to_all(coef_local, "seq", split_axis=0, concat_axis=2, tiled=True)
    filter_grad = coef_sum / math.sqrt(seq_total)
    prod_real = response[:, :, 0] * spec_gated[:, :, 0] + response[:, :, 1] * spec_gated[:, :, 1]
    prod_imag = response[:, :, 0] * spec_gated[:, :, 1] - response[:, :, 1] * spec_gated[:, :, 0]
    product = jnp.stack([prod_real, prod_imag], axis=2).astype(jnp.bfloat16)
    flat_product = product.reshape(width_share, nblocks, 2 * BLOCK)
    back_parts = jnp.einsum(
        "ckm,mj->ckj", flat_product, back_first, preferred_element_type=jnp.float32
    )
    back_parts = back_parts.reshape(width_share, nblocks, 2, BLOCK)
    back_twisted = twist_leading(back_parts, block_ids, all_inner, seq_total, 1.0).astype(
        jnp.bfloat16
    )
    time_field = jnp.einsum(
        "ckrm,krn->cnm", back_twisted, back_second, preferred_element_type=jnp.float32
    )
    time_field = time_field.reshape(width_share, seq_total).astype(jnp.bfloat16)
    home_field = lax.all_to_all(time_field, "seq", split_axis=1, concat_axis=0, tiled=True)
    conv_grad = home_field.T.astype(jnp.float32)
    normed_grad = conv_grad + skip_weight[None, :] * gated.astype(jnp.float32)
    scaled_grad = gain[None, :] * normed_grad
    row_dot = taken_together(jnp.sum(scaled_grad * upcast, axis=1), "ch")
    hidden_grad = (
        inverse_rms[:, None] * scaled_grad - upcast * (inverse_rms**3 * row_dot / D)[:, None]
    )
    return (hidden_grad.astype(jnp.bfloat16), filter_grad)


def solution(mesh):
    in_specs = (P("seq", "ch"), P("seq", "ch"), P("ch"), P("ch"), P(None, None, "ch"), P())
    out_specs = (P("seq", "ch"), P("seq", None, "ch"))
    return jax.shard_map(
        per_device, mesh=mesh, in_specs=in_specs, out_specs=out_specs, check_vma=False
    )
```

```python
import math

import jax
import jax.numpy as jnp
from jax import lax
from jax.sharding import PartitionSpec as P

D = 2048
BLOCK = 512
FEAT = 64


epsilon = 1e-06


def from_everyone(value, axis):
    copies = jnp.broadcast_to(value, (lax.axis_size(axis), *value.shape))
    return lax.all_to_all(copies, axis, split_axis=0, concat_axis=0, tiled=True)


def taken_together(value, axis):
    return lax.all_gather(value, axis).sum(axis=0)


def twin_table(count, sign):
    indices = jnp.arange(count, dtype=jnp.int32)
    product = indices[:, None] * indices[None, :] % count
    angles = 2.0 * math.pi / count * product.astype(jnp.float32)
    factor = 1.0 / math.sqrt(count)
    return (jnp.cos(angles) * factor, sign * jnp.sin(angles) * factor)


def block_matrix(count, sign):
    cosine, sine_part = twin_table(count, sign)
    upper = jnp.concatenate([cosine, sine_part], axis=1)
    lower = jnp.concatenate([-sine_part, cosine], axis=1)
    return jnp.concatenate([upper, lower], axis=0)


def twist_leading(parts, freq_index, pos_index, seq_total, sign):
    product = (freq_index[:, None] * pos_index[None, :]).astype(jnp.float32)
    angles = 2.0 * math.pi / seq_total * product
    cosine = jnp.cos(angles)[None, :, :]
    sine_part = (sign * jnp.sin(angles))[None, :, :]
    real_part = parts[:, :, 0] * cosine - parts[:, :, 1] * sine_part
    imag_part = parts[:, :, 0] * sine_part + parts[:, :, 1] * cosine
    return jnp.stack([real_part, imag_part], axis=2)


def features(freq_index, seq_total):
    orders = 2 * jnp.arange(FEAT, dtype=jnp.int32) + 1
    product = freq_index[..., None] * orders % seq_total
    return jnp.cos(2.0 * math.pi / seq_total * product.astype(jnp.float32))


def feature_factors(inner, nblocks, seq_total):
    orders = 2 * jnp.arange(FEAT, dtype=jnp.int32) + 1
    inner_ids = jnp.arange(inner, dtype=jnp.int32)
    block_ids = jnp.arange(nblocks, dtype=jnp.int32)
    inner_prod = (inner_ids[:, None] * orders[None, :]) % inner
    block_prod = (block_ids[:, None] * orders[None, :]) % seq_total
    inner_ang = 2.0 * math.pi / inner * inner_prod.astype(jnp.float32)
    block_ang = 2.0 * math.pi / seq_total * block_prod.astype(jnp.float32)
    inner_tab = jnp.concatenate([jnp.cos(inner_ang), jnp.sin(inner_ang)], axis=1)
    return inner_tab, jnp.cos(block_ang), jnp.sin(block_ang)


def per_device(hidden_in, grad_out, norm_gain, skip_weight, filter_coef, run_lengths):
    local_tokens = hidden_in.shape[0]
    local_width = hidden_in.shape[1]
    seq_parts = lax.axis_size("seq")
    seq_rank = lax.axis_index("seq")
    seq_total = local_tokens * seq_parts
    nblocks = seq_total // BLOCK
    upcast = hidden_in.astype(jnp.float32)
    square_sums = taken_together(jnp.sum(upcast * upcast, axis=1), "ch")
    inverse_rms = lax.rsqrt(square_sums / D + epsilon)
    gain = norm_gain.astype(jnp.float32)
    normed = (upcast * inverse_rms[:, None] * gain[None, :]).astype(jnp.bfloat16)
    run_ends = jnp.cumsum(run_lengths)
    positions = seq_rank * local_tokens + jnp.arange(local_tokens, dtype=jnp.int32)
    run_index = jnp.sum((run_ends[None, :] <= positions[:, None]).astype(jnp.int32), axis=1)
    keep = run_index % 2 == 0
    gated = jnp.where(keep[:, None], grad_out, jnp.zeros_like(grad_out))
    forward_first = jnp.stack(twin_table(nblocks, -1.0), axis=2).astype(jnp.bfloat16)
    forward_second = block_matrix(BLOCK, -1.0).astype(jnp.bfloat16)
    back_first = block_matrix(BLOCK, 1.0).astype(jnp.bfloat16)
    cosine, sine_part = twin_table(nblocks, 1.0)
    back_second = jnp.stack([cosine, -sine_part], axis=1).astype(jnp.bfloat16)
    block_ids = jnp.arange(nblocks, dtype=jnp.int32)
    all_inner = jnp.arange(BLOCK, dtype=jnp.int32)
    width_share = local_width // seq_parts
    gated_moved = lax.all_to_all(gated.T, "seq", split_axis=0, concat_axis=1, tiled=True)
    gated_moved, normed = lax.optimization_barrier((gated_moved, normed))
    normed_moved = lax.all_to_all(normed.T, "seq", split_axis=0, concat_axis=1, tiled=True)
    moved = (normed_moved, gated_moved)
    coef_part = lax.dynamic_slice_in_dim(filter_coef, seq_rank * width_share, width_share, 2)

    def local_freq(field):
        blocks = field.reshape(width_share, nblocks, BLOCK)
        parts = jnp.einsum(
            "cnm,nkr->ckrm", blocks, forward_first, preferred_element_type=jnp.float32
        )
        turned = twist_leading(parts, block_ids, all_inner, seq_total, -1.0).astype(jnp.bfloat16)
        flat = turned.reshape(width_share, nblocks, 2 * BLOCK)
        spectrum = jnp.einsum(
            "ckm,mj->ckj", flat, forward_second, preferred_element_type=jnp.float32
        )
        return spectrum.reshape(width_share, nblocks, 2, BLOCK)

    spec_gated = local_freq(moved[1])
    inner_tab, block_cos, block_sin = feature_factors(BLOCK, nblocks, seq_total)
    coef_t = coef_part.astype(jnp.float32).transpose(2, 1, 0)[:, None, :, :]
    coef_mix = jnp.concatenate(
        [block_cos[None, :, None, :] * coef_t, -block_sin[None, :, None, :] * coef_t], axis=3
    )
    response = jnp.einsum(
        "ckrj,bj->ckrb", coef_mix, inner_tab,
        precision=lax.Precision.HIGHEST, preferred_element_type=jnp.float32,
    )
    prod_real = response[:, :, 0] * spec_gated[:, :, 0] + response[:, :, 1] * spec_gated[:, :, 1]
    prod_imag = response[:, :, 0] * spec_gated[:, :, 1] - response[:, :, 1] * spec_gated[:, :, 0]
    product = jnp.stack([prod_real, prod_imag], axis=2).astype(jnp.bfloat16)
    flat_product = product.reshape(width_share, nblocks, 2 * BLOCK)
    back_parts = jnp.einsum(
        "ckm,mj->ckj", flat_product, back_first, preferred_element_type=jnp.float32
    )
    back_parts = back_parts.reshape(width_share, nblocks, 2, BLOCK)
    back_twisted = twist_leading(back_parts, block_ids, all_inner, seq_total, 1.0).astype(
        jnp.bfloat16
    )
    time_field = jnp.einsum(
        "ckrm,krn->cnm", back_twisted, back_second, preferred_element_type=jnp.float32
    )
    time_field = time_field.reshape(width_share, seq_total).astype(jnp.bfloat16)
    time_field, normed_moved = lax.optimization_barrier((time_field, normed_moved))
    spec_normed = local_freq(normed_moved)
    grad_real = (
        spec_normed[:, :, 0] * spec_gated[:, :, 0] + spec_normed[:, :, 1] * spec_gated[:, :, 1]
    )
    grad_imag = (
        spec_normed[:, :, 0] * spec_gated[:, :, 1] - spec_normed[:, :, 1] * spec_gated[:, :, 0]
    )
    spec_grad = jnp.stack([grad_real, grad_imag], axis=2).astype(jnp.bfloat16)
    partial = jnp.einsum(
        "ckrb,bj->ckrj", spec_grad.astype(jnp.float32), inner_tab,
        precision=lax.Precision.HIGHEST, preferred_element_type=jnp.float32,
    )
    coef_local = jnp.einsum(
        "ckrj,kj->jrc", partial[..., :FEAT], block_cos, precision=lax.Precision.HIGHEST
    ) - jnp.einsum(
        "ckrj,kj->jrc", partial[..., FEAT:], block_sin, precision=lax.Precision.HIGHEST
    )
    coef_full = jnp.zeros((FEAT, 2, local_width), jnp.float32)
    coef_full = lax.dynamic_update_slice_in_dim(coef_full, coef_local, seq_rank * width_share, 2)
    coef_sum = lax.psum_scatter(coef_full, "seq", scatter_dimension=0, tiled=True)
    filter_grad = coef_sum / math.sqrt(seq_total)
    home_field = lax.all_to_all(time_field, "seq", split_axis=1, concat_axis=0, tiled=True)
    conv_grad = home_field.T.astype(jnp.float32)
    normed_grad = conv_grad + skip_weight[None, :] * gated.astype(jnp.float32)
    scaled_grad = gain[None, :] * normed_grad
    row_dot = taken_together(jnp.sum(scaled_grad * upcast, axis=1), "ch")
    hidden_grad = (
        inverse_rms[:, None] * scaled_grad - upcast * (inverse_rms**3 * row_dot / D)[:, None]
    )
    return (hidden_grad.astype(jnp.bfloat16), filter_grad)


def solution(mesh):
    in_specs = (P("seq", "ch"), P("seq", "ch"), P("ch"), P("ch"), P(None, None, "ch"), P())
    out_specs = (P("seq", "ch"), P("seq", None, "ch"))
    return jax.shard_map(
        per_device, mesh=mesh, in_specs=in_specs, out_specs=out_specs, check_vma=False
    )
```

```python
import math

import jax
import jax.numpy as jnp
from jax import lax
from jax.sharding import PartitionSpec as P

D = 2048
BLOCK = 512
FEAT = 64


epsilon = 1e-06


def from_everyone(value, axis):
    copies = jnp.broadcast_to(value, (lax.axis_size(axis), *value.shape))
    return lax.all_to_all(copies, axis, split_axis=0, concat_axis=0, tiled=True)


def taken_together(value, axis):
    return lax.all_gather(value, axis).sum(axis=0)


def twin_table(count, sign):
    low = 64 if count % 64 == 0 else count
    indices = jnp.arange(count, dtype=jnp.int32)
    low_ids = jnp.arange(low, dtype=jnp.int32)
    high_ids = jnp.arange(count // low, dtype=jnp.int32) * low
    low_ang = 2.0 * math.pi / count * (indices[:, None] * low_ids[None, :] % count).astype(jnp.float32)
    high_ang = 2.0 * math.pi / count * (indices[:, None] * high_ids[None, :] % count).astype(jnp.float32)
    low_cos, low_sin = jnp.cos(low_ang)[:, None, :], jnp.sin(low_ang)[:, None, :]
    high_cos, high_sin = jnp.cos(high_ang)[:, :, None], jnp.sin(high_ang)[:, :, None]
    cosine = (low_cos * high_cos - low_sin * high_sin).reshape(count, count)
    sine = (low_sin * high_cos + low_cos * high_sin).reshape(count, count)
    factor = 1.0 / math.sqrt(count)
    return (cosine * factor, sign * sine * factor)


def block_matrix(count, sign):
    cosine, sine_part = twin_table(count, sign)
    half = jnp.arange(2, dtype=jnp.int32)
    same = (half[:, None, None, None] == half[None, None, :, None])
    upper = half[:, None, None, None] == 0
    sine_signed = jnp.where(upper, sine_part[None, :, None, :], -sine_part[None, :, None, :])
    whole = jnp.where(same, cosine[None, :, None, :], sine_signed)
    return whole.reshape(2 * count, 2 * count)


def twist_leading(parts, freq_index, pos_index, seq_total, sign):
    product = (freq_index[:, None] * pos_index[None, :]).astype(jnp.float32)
    angles = 2.0 * math.pi / seq_total * product
    cosine = jnp.cos(angles)[None, :, :]
    sine_part = (sign * jnp.sin(angles))[None, :, :]
    real_part = parts[:, :, 0] * cosine - parts[:, :, 1] * sine_part
    imag_part = parts[:, :, 0] * sine_part + parts[:, :, 1] * cosine
    return jnp.stack([real_part, imag_part], axis=2)


def features(freq_index, seq_total):
    orders = 2 * jnp.arange(FEAT, dtype=jnp.int32) + 1
    product = freq_index[..., None] * orders % seq_total
    return jnp.cos(2.0 * math.pi / seq_total * product.astype(jnp.float32))


def feature_factors(inner, nblocks, seq_total):
    orders = 2 * jnp.arange(FEAT, dtype=jnp.int32) + 1
    inner_ids = jnp.arange(inner, dtype=jnp.int32)
    block_ids = jnp.arange(nblocks, dtype=jnp.int32)
    inner_prod = (inner_ids[:, None] * orders[None, :]) % inner
    block_prod = (block_ids[:, None] * orders[None, :]) % seq_total
    inner_ang = 2.0 * math.pi / inner * inner_prod.astype(jnp.float32)
    block_ang = 2.0 * math.pi / seq_total * block_prod.astype(jnp.float32)
    inner_tab = jnp.concatenate([jnp.cos(inner_ang), jnp.sin(inner_ang)], axis=1)
    return inner_tab, jnp.cos(block_ang), jnp.sin(block_ang)


def per_device(hidden_in, grad_out, norm_gain, skip_weight, filter_coef, run_lengths):
    local_tokens = hidden_in.shape[0]
    local_width = hidden_in.shape[1]
    seq_parts = lax.axis_size("seq")
    seq_rank = lax.axis_index("seq")
    seq_total = local_tokens * seq_parts
    nblocks = seq_total // BLOCK
    upcast = hidden_in.astype(jnp.float32)
    square_sums = taken_together(jnp.sum(upcast * upcast, axis=1), "ch")
    inverse_rms = lax.rsqrt(square_sums / D + epsilon)
    gain = norm_gain.astype(jnp.float32)
    normed = (upcast * inverse_rms[:, None] * gain[None, :]).astype(jnp.bfloat16)
    run_ends = jnp.cumsum(run_lengths)
    positions = seq_rank * local_tokens + jnp.arange(local_tokens, dtype=jnp.int32)
    run_index = jnp.sum((run_ends[None, :] <= positions[:, None]).astype(jnp.int32), axis=1)
    keep = run_index % 2 == 0
    gated = jnp.where(keep[:, None], grad_out, jnp.zeros_like(grad_out))
    forward_first = jnp.stack(twin_table(nblocks, -1.0), axis=2).astype(jnp.bfloat16)
    forward_second = block_matrix(BLOCK, -1.0).astype(jnp.bfloat16)
    back_first = block_matrix(BLOCK, 1.0).astype(jnp.bfloat16)
    cosine, sine_part = twin_table(nblocks, 1.0)
    back_second = jnp.stack([cosine, -sine_part], axis=1).astype(jnp.bfloat16)
    block_ids = jnp.arange(nblocks, dtype=jnp.int32)
    all_inner = jnp.arange(BLOCK, dtype=jnp.int32)
    width_share = local_width // seq_parts
    gated_moved = lax.all_to_all(gated.T, "seq", split_axis=0, concat_axis=1, tiled=True)
    gated_moved, normed = lax.optimization_barrier((gated_moved, normed))
    normed_moved = lax.all_to_all(normed.T, "seq", split_axis=0, concat_axis=1, tiled=True)
    moved = (normed_moved, gated_moved)
    coef_part = lax.dynamic_slice_in_dim(filter_coef, seq_rank * width_share, width_share, 2)

    def local_freq(field):
        blocks = field.reshape(width_share, nblocks, BLOCK)
        parts = jnp.einsum(
            "cnm,nkr->ckrm", blocks, forward_first, preferred_element_type=jnp.float32
        )
        turned = twist_leading(parts, block_ids, all_inner, seq_total, -1.0).astype(jnp.bfloat16)
        flat = turned.reshape(width_share, nblocks, 2 * BLOCK)
        spectrum = jnp.einsum(
            "ckm,mj->ckj", flat, forward_second, preferred_element_type=jnp.float32
        )
        return spectrum.reshape(width_share, nblocks, 2, BLOCK)

    spec_gated = local_freq(moved[1])
    inner_tab, block_cos, block_sin = feature_factors(BLOCK, nblocks, seq_total)
    coef_t = coef_part.astype(jnp.float32).transpose(2, 1, 0)[:, None, :, :]
    coef_mix = jnp.concatenate(
        [block_cos[None, :, None, :] * coef_t, -block_sin[None, :, None, :] * coef_t], axis=3
    )
    response = jnp.einsum(
        "ckrj,bj->ckrb", coef_mix, inner_tab,
        precision=lax.Precision.HIGHEST, preferred_element_type=jnp.float32,
    )
    prod_real = response[:, :, 0] * spec_gated[:, :, 0] + response[:, :, 1] * spec_gated[:, :, 1]
    prod_imag = response[:, :, 0] * spec_gated[:, :, 1] - response[:, :, 1] * spec_gated[:, :, 0]
    product = jnp.stack([prod_real, prod_imag], axis=2).astype(jnp.bfloat16)
    flat_product = product.reshape(width_share, nblocks, 2 * BLOCK)
    back_parts = jnp.einsum(
        "ckm,mj->ckj", flat_product, back_first, preferred_element_type=jnp.float32
    )
    back_parts = back_parts.reshape(width_share, nblocks, 2, BLOCK)
    back_twisted = twist_leading(back_parts, block_ids, all_inner, seq_total, 1.0).astype(
        jnp.bfloat16
    )
    time_field = jnp.einsum(
        "ckrm,krn->cnm", back_twisted, back_second, preferred_element_type=jnp.float32
    )
    time_field = time_field.reshape(width_share, seq_total).astype(jnp.bfloat16)
    time_field, normed_moved = lax.optimization_barrier((time_field, normed_moved))
    spec_normed = local_freq(normed_moved)
    grad_real = (
        spec_normed[:, :, 0] * spec_gated[:, :, 0] + spec_normed[:, :, 1] * spec_gated[:, :, 1]
    )
    grad_imag = (
        spec_normed[:, :, 0] * spec_gated[:, :, 1] - spec_normed[:, :, 1] * spec_gated[:, :, 0]
    )
    spec_grad = jnp.stack([grad_real, grad_imag], axis=2).astype(jnp.bfloat16)
    partial = jnp.einsum(
        "ckrb,bj->ckrj", spec_grad.astype(jnp.float32), inner_tab,
        precision=lax.Precision.HIGHEST, preferred_element_type=jnp.float32,
    )
    coef_local = jnp.einsum(
        "ckrj,kj->jrc", partial[..., :FEAT], block_cos, precision=lax.Precision.HIGHEST
    ) - jnp.einsum(
        "ckrj,kj->jrc", partial[..., FEAT:], block_sin, precision=lax.Precision.HIGHEST
    )
    home_field = lax.all_to_all(time_field, "seq", split_axis=1, concat_axis=0, tiled=True)
    coef_local, home_field = lax.optimization_barrier((coef_local, home_field))
    coef_sum = lax.all_to_all(coef_local, "seq", split_axis=0, concat_axis=2, tiled=True)
    filter_grad = coef_sum / math.sqrt(seq_total)
    conv_grad = home_field.T.astype(jnp.float32)
    normed_grad = conv_grad + skip_weight[None, :] * gated.astype(jnp.float32)
    scaled_grad = gain[None, :] * normed_grad
    row_dot = taken_together(jnp.sum(scaled_grad * upcast, axis=1), "ch")
    hidden_grad = (
        inverse_rms[:, None] * scaled_grad - upcast * (inverse_rms**3 * row_dot / D)[:, None]
    )
    return (hidden_grad.astype(jnp.bfloat16), filter_grad)


def solution(mesh):
    in_specs = (P("seq", "ch"), P("seq", "ch"), P("ch"), P("ch"), P(None, None, "ch"), P())
    out_specs = (P("seq", "ch"), P("seq", None, "ch"))
    return jax.shard_map(
        per_device, mesh=mesh, in_specs=in_specs, out_specs=out_specs, check_vma=False
    )
```

```python
import math

import jax
import jax.numpy as jnp
from jax import lax
from jax.sharding import PartitionSpec as P

D = 2048
BLOCK = 512
FEAT = 64


epsilon = 1e-06


def from_everyone(value, axis):
    copies = jnp.broadcast_to(value, (lax.axis_size(axis), *value.shape))
    return lax.all_to_all(copies, axis, split_axis=0, concat_axis=0, tiled=True)


def taken_together(value, axis):
    return from_everyone(value, axis).sum(axis=0)


def twin_table(count, sign):
    low = 64 if count % 64 == 0 else count
    indices = jnp.arange(count, dtype=jnp.int32)
    low_ids = jnp.arange(low, dtype=jnp.int32)
    high_ids = jnp.arange(count // low, dtype=jnp.int32) * low
    low_ang = 2.0 * math.pi / count * (indices[:, None] * low_ids[None, :] % count).astype(jnp.float32)
    high_ang = 2.0 * math.pi / count * (indices[:, None] * high_ids[None, :] % count).astype(jnp.float32)
    low_cos, low_sin = jnp.cos(low_ang)[:, None, :], jnp.sin(low_ang)[:, None, :]
    high_cos, high_sin = jnp.cos(high_ang)[:, :, None], jnp.sin(high_ang)[:, :, None]
    cosine = (low_cos * high_cos - low_sin * high_sin).reshape(count, count)
    sine = (low_sin * high_cos + low_cos * high_sin).reshape(count, count)
    factor = 1.0 / math.sqrt(count)
    return (cosine * factor, sign * sine * factor)


def block_matrix(count, sign):
    cosine, sine_part = twin_table(count, sign)
    half = jnp.arange(2, dtype=jnp.int32)
    same = (half[:, None, None, None] == half[None, None, :, None])
    upper = half[:, None, None, None] == 0
    sine_signed = jnp.where(upper, sine_part[None, :, None, :], -sine_part[None, :, None, :])
    whole = jnp.where(same, cosine[None, :, None, :], sine_signed)
    return whole.reshape(2 * count, 2 * count)


def twist_leading(parts, freq_index, pos_index, seq_total, sign):
    product = (freq_index[:, None] * pos_index[None, :]).astype(jnp.float32)
    angles = 2.0 * math.pi / seq_total * product
    cosine = jnp.cos(angles)[None, :, :]
    sine_part = (sign * jnp.sin(angles))[None, :, :]
    real_part = parts[:, :, 0] * cosine - parts[:, :, 1] * sine_part
    imag_part = parts[:, :, 0] * sine_part + parts[:, :, 1] * cosine
    return jnp.stack([real_part, imag_part], axis=2)


def features(freq_index, seq_total):
    orders = 2 * jnp.arange(FEAT, dtype=jnp.int32) + 1
    product = freq_index[..., None] * orders % seq_total
    return jnp.cos(2.0 * math.pi / seq_total * product.astype(jnp.float32))


def feature_factors(inner, nblocks, seq_total):
    orders = 2 * jnp.arange(FEAT, dtype=jnp.int32) + 1
    inner_ids = jnp.arange(inner, dtype=jnp.int32)
    block_ids = jnp.arange(nblocks, dtype=jnp.int32)
    inner_prod = (inner_ids[:, None] * orders[None, :]) % inner
    block_prod = (block_ids[:, None] * orders[None, :]) % seq_total
    inner_ang = 2.0 * math.pi / inner * inner_prod.astype(jnp.float32)
    block_ang = 2.0 * math.pi / seq_total * block_prod.astype(jnp.float32)
    inner_tab = jnp.concatenate([jnp.cos(inner_ang), jnp.sin(inner_ang)], axis=1)
    return inner_tab, jnp.cos(block_ang), jnp.sin(block_ang)


def per_device(hidden_in, grad_out, norm_gain, skip_weight, filter_coef, run_lengths):
    local_tokens = hidden_in.shape[0]
    local_width = hidden_in.shape[1]
    seq_parts = lax.axis_size("seq")
    seq_rank = lax.axis_index("seq")
    seq_total = local_tokens * seq_parts
    nblocks = seq_total // BLOCK
    upcast = hidden_in.astype(jnp.float32)
    square_sums = taken_together(jnp.sum(upcast * upcast, axis=1), "ch")
    inverse_rms = lax.rsqrt(square_sums / D + epsilon)
    gain = norm_gain.astype(jnp.float32)
    normed = (upcast * inverse_rms[:, None] * gain[None, :]).astype(jnp.bfloat16)
    run_ends = jnp.cumsum(run_lengths)
    positions = seq_rank * local_tokens + jnp.arange(local_tokens, dtype=jnp.int32)
    run_index = jnp.sum((run_ends[None, :] <= positions[:, None]).astype(jnp.int32), axis=1)
    keep = run_index % 2 == 0
    gated = jnp.where(keep[:, None], grad_out, jnp.zeros_like(grad_out))
    forward_first = jnp.stack(twin_table(nblocks, -1.0), axis=2).astype(jnp.bfloat16)
    forward_second = block_matrix(BLOCK, -1.0).astype(jnp.bfloat16)
    back_first = block_matrix(BLOCK, 1.0).astype(jnp.bfloat16)
    cosine, sine_part = twin_table(nblocks, 1.0)
    back_second = jnp.stack([cosine, -sine_part], axis=1).astype(jnp.bfloat16)
    block_ids = jnp.arange(nblocks, dtype=jnp.int32)
    all_inner = jnp.arange(BLOCK, dtype=jnp.int32)
    width_share = local_width // seq_parts
    gated, inverse_rms = lax.optimization_barrier((gated, inverse_rms))
    gated_moved = lax.all_to_all(gated.T, "seq", split_axis=0, concat_axis=1, tiled=True)
    gated_moved, normed = lax.optimization_barrier((gated_moved, normed))
    normed_moved = lax.all_to_all(normed.T, "seq", split_axis=0, concat_axis=1, tiled=True)
    moved = (normed_moved, gated_moved)
    coef_part = lax.dynamic_slice_in_dim(filter_coef, seq_rank * width_share, width_share, 2)

    def local_freq(field):
        blocks = field.reshape(width_share, nblocks, BLOCK)
        parts = jnp.einsum(
            "cnm,nkr->ckrm", blocks, forward_first, preferred_element_type=jnp.float32
        )
        turned = twist_leading(parts, block_ids, all_inner, seq_total, -1.0).astype(jnp.bfloat16)
        flat = turned.reshape(width_share, nblocks, 2 * BLOCK)
        spectrum = jnp.einsum(
            "ckm,mj->ckj", flat, forward_second, preferred_element_type=jnp.float32
        )
        return spectrum.reshape(width_share, nblocks, 2, BLOCK)

    spec_gated = local_freq(moved[1])
    inner_tab, block_cos, block_sin = feature_factors(BLOCK, nblocks, seq_total)
    coef_t = coef_part.astype(jnp.float32).transpose(2, 1, 0)[:, None, :, :]
    coef_mix = jnp.concatenate(
        [block_cos[None, :, None, :] * coef_t, -block_sin[None, :, None, :] * coef_t], axis=3
    )
    response = jnp.einsum(
        "ckrj,bj->ckrb", coef_mix, inner_tab,
        precision=lax.Precision.HIGHEST, preferred_element_type=jnp.float32,
    )
    prod_real = response[:, :, 0] * spec_gated[:, :, 0] + response[:, :, 1] * spec_gated[:, :, 1]
    prod_imag = response[:, :, 0] * spec_gated[:, :, 1] - response[:, :, 1] * spec_gated[:, :, 0]
    product = jnp.stack([prod_real, prod_imag], axis=2).astype(jnp.bfloat16)
    flat_product = product.reshape(width_share, nblocks, 2 * BLOCK)
    back_parts = jnp.einsum(
        "ckm,mj->ckj", flat_product, back_first, preferred_element_type=jnp.float32
    )
    back_parts = back_parts.reshape(width_share, nblocks, 2, BLOCK)
    back_twisted = twist_leading(back_parts, block_ids, all_inner, seq_total, 1.0).astype(
        jnp.bfloat16
    )
    time_field = jnp.einsum(
        "ckrm,krn->cnm", back_twisted, back_second, preferred_element_type=jnp.float32
    )
    time_field = time_field.reshape(width_share, seq_total).astype(jnp.bfloat16)
    time_field, normed_moved = lax.optimization_barrier((time_field, normed_moved))
    spec_normed = local_freq(normed_moved)
    grad_real = (
        spec_normed[:, :, 0] * spec_gated[:, :, 0] + spec_normed[:, :, 1] * spec_gated[:, :, 1]
    )
    grad_imag = (
        spec_normed[:, :, 0] * spec_gated[:, :, 1] - spec_normed[:, :, 1] * spec_gated[:, :, 0]
    )
    spec_grad = jnp.stack([grad_real, grad_imag], axis=2).astype(jnp.bfloat16)
    partial = jnp.einsum(
        "ckrb,bj->ckrj", spec_grad.astype(jnp.float32), inner_tab,
        precision=lax.Precision.HIGHEST, preferred_element_type=jnp.float32,
    )
    coef_local = jnp.sum(
        partial[..., :FEAT] * block_cos[None, :, None, :]
        - partial[..., FEAT:] * block_sin[None, :, None, :],
        axis=1,
    ).transpose(2, 1, 0)
    home_field = lax.all_to_all(time_field, "seq", split_axis=1, concat_axis=0, tiled=True)
    coef_rows = FEAT // seq_parts
    coef_all = lax.all_gather(coef_local, "seq")
    coef_all = lax.dynamic_slice_in_dim(coef_all, seq_rank * coef_rows, coef_rows, 1)
    coef_sum = coef_all.transpose(1, 2, 0, 3).reshape(coef_rows, 2, local_width)
    coef_sum, home_field = lax.optimization_barrier((coef_sum, home_field))
    filter_grad = coef_sum / math.sqrt(seq_total)
    conv_grad = home_field.T.astype(jnp.float32)
    normed_grad = conv_grad + skip_weight[None, :] * gated.astype(jnp.float32)
    scaled_grad = gain[None, :] * normed_grad
    row_dot = taken_together(jnp.sum(scaled_grad * upcast, axis=1), "ch")
    hidden_grad = (
        inverse_rms[:, None] * scaled_grad - upcast * (inverse_rms**3 * row_dot / D)[:, None]
    )
    return (hidden_grad.astype(jnp.bfloat16), filter_grad)


def solution(mesh):
    in_specs = (P("seq", "ch"), P("seq", "ch"), P("ch"), P("ch"), P(None, None, "ch"), P())
    out_specs = (P("seq", "ch"), P("seq", None, "ch"))
    return jax.shard_map(
        per_device, mesh=mesh, in_specs=in_specs, out_specs=out_specs, check_vma=False
    )
```

```python
import math

import jax
import jax.numpy as jnp
from jax import lax
from jax.sharding import PartitionSpec as P

D = 2048
BLOCK = 512
FEAT = 64


epsilon = 1e-06


def from_everyone(value, axis):
    copies = jnp.broadcast_to(value, (lax.axis_size(axis), *value.shape))
    return lax.all_to_all(copies, axis, split_axis=0, concat_axis=0, tiled=True)


def taken_together(value, axis):
    count = lax.axis_size(axis)
    step = 1
    while step < count:
        pairs = [(i, i ^ step) for i in range(count)]
        value = value + lax.ppermute(value, axis, pairs)
        step *= 2
    return value


def twin_table(count, sign):
    low = 64 if count % 64 == 0 else count
    indices = jnp.arange(count, dtype=jnp.int32)
    low_ids = jnp.arange(low, dtype=jnp.int32)
    high_ids = jnp.arange(count // low, dtype=jnp.int32) * low
    low_ang = 2.0 * math.pi / count * (indices[:, None] * low_ids[None, :] % count).astype(jnp.float32)
    high_ang = 2.0 * math.pi / count * (indices[:, None] * high_ids[None, :] % count).astype(jnp.float32)
    low_cos, low_sin = jnp.cos(low_ang)[:, None, :], jnp.sin(low_ang)[:, None, :]
    high_cos, high_sin = jnp.cos(high_ang)[:, :, None], jnp.sin(high_ang)[:, :, None]
    cosine = (low_cos * high_cos - low_sin * high_sin).reshape(count, count)
    sine = (low_sin * high_cos + low_cos * high_sin).reshape(count, count)
    factor = 1.0 / math.sqrt(count)
    return (cosine * factor, sign * sine * factor)


def block_matrix(count, sign):
    cosine, sine_part = twin_table(count, sign)
    half = jnp.arange(2, dtype=jnp.int32)
    same = (half[:, None, None, None] == half[None, None, :, None])
    upper = half[:, None, None, None] == 0
    sine_signed = jnp.where(upper, sine_part[None, :, None, :], -sine_part[None, :, None, :])
    whole = jnp.where(same, cosine[None, :, None, :], sine_signed)
    return whole.reshape(2 * count, 2 * count)


def twist_leading(parts, freq_index, pos_index, seq_total, sign):
    product = (freq_index[:, None] * pos_index[None, :]).astype(jnp.float32)
    angles = 2.0 * math.pi / seq_total * product
    cosine = jnp.cos(angles)[None, :, :]
    sine_part = (sign * jnp.sin(angles))[None, :, :]
    real_part = parts[:, :, 0] * cosine - parts[:, :, 1] * sine_part
    imag_part = parts[:, :, 0] * sine_part + parts[:, :, 1] * cosine
    return jnp.stack([real_part, imag_part], axis=2)


def features(freq_index, seq_total):
    orders = 2 * jnp.arange(FEAT, dtype=jnp.int32) + 1
    product = freq_index[..., None] * orders % seq_total
    return jnp.cos(2.0 * math.pi / seq_total * product.astype(jnp.float32))


def feature_factors(inner, nblocks, seq_total):
    orders = 2 * jnp.arange(FEAT, dtype=jnp.int32) + 1
    inner_ids = jnp.arange(inner, dtype=jnp.int32)
    block_ids = jnp.arange(nblocks, dtype=jnp.int32)
    inner_prod = (inner_ids[:, None] * orders[None, :]) % inner
    block_prod = (block_ids[:, None] * orders[None, :]) % seq_total
    inner_ang = 2.0 * math.pi / inner * inner_prod.astype(jnp.float32)
    block_ang = 2.0 * math.pi / seq_total * block_prod.astype(jnp.float32)
    inner_tab = jnp.concatenate([jnp.cos(inner_ang), jnp.sin(inner_ang)], axis=1)
    return inner_tab, jnp.cos(block_ang), jnp.sin(block_ang)


def per_device(hidden_in, grad_out, norm_gain, skip_weight, filter_coef, run_lengths):
    local_tokens = hidden_in.shape[0]
    local_width = hidden_in.shape[1]
    seq_parts = lax.axis_size("seq")
    seq_rank = lax.axis_index("seq")
    seq_total = local_tokens * seq_parts
    nblocks = seq_total // BLOCK
    upcast = hidden_in.astype(jnp.float32)
    square_sums = taken_together(jnp.sum(upcast * upcast, axis=1), "ch")
    inverse_rms = lax.rsqrt(square_sums / D + epsilon)
    gain = norm_gain.astype(jnp.float32)
    normed = (upcast * inverse_rms[:, None] * gain[None, :]).astype(jnp.bfloat16)
    run_ends = jnp.cumsum(run_lengths)
    positions = seq_rank * local_tokens + jnp.arange(local_tokens, dtype=jnp.int32)
    run_index = jnp.sum((run_ends[None, :] <= positions[:, None]).astype(jnp.int32), axis=1)
    keep = run_index % 2 == 0
    gated = jnp.where(keep[:, None], grad_out, jnp.zeros_like(grad_out))
    forward_first = jnp.stack(twin_table(nblocks, -1.0), axis=2).astype(jnp.bfloat16)
    forward_second = block_matrix(BLOCK, -1.0).astype(jnp.bfloat16)
    back_first = block_matrix(BLOCK, 1.0).astype(jnp.bfloat16)
    cosine, sine_part = twin_table(nblocks, 1.0)
    back_second = jnp.stack([cosine, -sine_part], axis=1).astype(jnp.bfloat16)
    block_ids = jnp.arange(nblocks, dtype=jnp.int32)
    all_inner = jnp.arange(BLOCK, dtype=jnp.int32)
    width_share = local_width // seq_parts
    gated_moved = lax.all_to_all(gated.T, "seq", split_axis=0, concat_axis=1, tiled=True)
    gated_moved, normed = lax.optimization_barrier((gated_moved, normed))
    normed_moved = lax.all_to_all(normed.T, "seq", split_axis=0, concat_axis=1, tiled=True)
    moved = (normed_moved, gated_moved)
    coef_part = lax.dynamic_slice_in_dim(filter_coef, seq_rank * width_share, width_share, 2)

    def local_freq(field):
        blocks = field.reshape(width_share, nblocks, BLOCK)
        parts = jnp.einsum(
            "cnm,nkr->ckrm", blocks, forward_first, preferred_element_type=jnp.float32
        )
        turned = twist_leading(parts, block_ids, all_inner, seq_total, -1.0).astype(jnp.bfloat16)
        flat = turned.reshape(width_share, nblocks, 2 * BLOCK)
        spectrum = jnp.einsum(
            "ckm,mj->ckj", flat, forward_second, preferred_element_type=jnp.float32
        )
        return spectrum.reshape(width_share, nblocks, 2, BLOCK)

    spec_gated = local_freq(moved[1])
    inner_tab, block_cos, block_sin = feature_factors(BLOCK, nblocks, seq_total)
    coef_t = coef_part.astype(jnp.float32).transpose(2, 1, 0)[:, None, :, :]
    coef_mix = jnp.concatenate(
        [block_cos[None, :, None, :] * coef_t, -block_sin[None, :, None, :] * coef_t], axis=3
    )
    response = jnp.einsum(
        "ckrj,bj->ckrb", coef_mix, inner_tab,
        precision=lax.Precision.HIGHEST, preferred_element_type=jnp.float32,
    )
    prod_real = response[:, :, 0] * spec_gated[:, :, 0] + response[:, :, 1] * spec_gated[:, :, 1]
    prod_imag = response[:, :, 0] * spec_gated[:, :, 1] - response[:, :, 1] * spec_gated[:, :, 0]
    product = jnp.stack([prod_real, prod_imag], axis=2).astype(jnp.bfloat16)
    flat_product = product.reshape(width_share, nblocks, 2 * BLOCK)
    back_parts = jnp.einsum(
        "ckm,mj->ckj", flat_product, back_first, preferred_element_type=jnp.float32
    )
    back_parts = back_parts.reshape(width_share, nblocks, 2, BLOCK)
    back_twisted = twist_leading(back_parts, block_ids, all_inner, seq_total, 1.0).astype(
        jnp.bfloat16
    )
    time_field = jnp.einsum(
        "ckrm,krn->cnm", back_twisted, back_second, preferred_element_type=jnp.float32
    )
    time_field = time_field.reshape(width_share, seq_total).astype(jnp.bfloat16)
    time_field, normed_moved = lax.optimization_barrier((time_field, normed_moved))
    spec_normed = local_freq(normed_moved)
    grad_real = (
        spec_normed[:, :, 0] * spec_gated[:, :, 0] + spec_normed[:, :, 1] * spec_gated[:, :, 1]
    )
    grad_imag = (
        spec_normed[:, :, 0] * spec_gated[:, :, 1] - spec_normed[:, :, 1] * spec_gated[:, :, 0]
    )
    spec_grad = jnp.stack([grad_real, grad_imag], axis=2).astype(jnp.bfloat16)
    partial = jnp.einsum(
        "ckrb,bj->ckrj", spec_grad.astype(jnp.float32), inner_tab,
        precision=lax.Precision.HIGHEST, preferred_element_type=jnp.float32,
    )
    coef_local = jnp.sum(
        partial[..., :FEAT] * block_cos[None, :, None, :]
        - partial[..., FEAT:] * block_sin[None, :, None, :],
        axis=1,
    ).transpose(2, 1, 0)
    home_field = lax.all_to_all(time_field, "seq", split_axis=1, concat_axis=0, tiled=True)
    coef_local, home_field = lax.optimization_barrier((coef_local, home_field))
    coef_sum = lax.all_to_all(coef_local, "seq", split_axis=0, concat_axis=2, tiled=True)
    filter_grad = coef_sum / math.sqrt(seq_total)
    conv_grad = home_field.T.astype(jnp.float32)
    normed_grad = conv_grad + skip_weight[None, :] * gated.astype(jnp.float32)
    scaled_grad = gain[None, :] * normed_grad
    row_dot = taken_together(jnp.sum(scaled_grad * upcast, axis=1), "ch")
    hidden_grad = (
        inverse_rms[:, None] * scaled_grad - upcast * (inverse_rms**3 * row_dot / D)[:, None]
    )
    return (hidden_grad.astype(jnp.bfloat16), filter_grad)


def solution(mesh):
    in_specs = (P("seq", "ch"), P("seq", "ch"), P("ch"), P("ch"), P(None, None, "ch"), P())
    out_specs = (P("seq", "ch"), P("seq", None, "ch"))
    return jax.shard_map(
        per_device, mesh=mesh, in_specs=in_specs, out_specs=out_specs, check_vma=False
    )
```

```python
import math

import jax
import jax.numpy as jnp
from jax import lax
from jax.sharding import PartitionSpec as P

D = 2048
BLOCK = 512
FEAT = 64


epsilon = 1e-06


def from_everyone(value, axis):
    copies = jnp.broadcast_to(value, (lax.axis_size(axis), *value.shape))
    return lax.all_to_all(copies, axis, split_axis=0, concat_axis=0, tiled=True)


def taken_together(value, axis):
    count = lax.axis_size(axis)
    step = 1
    while step < count:
        pairs = [(i, i ^ step) for i in range(count)]
        value = value + lax.ppermute(value, axis, pairs)
        step *= 2
    return value


def spread_blocks(blocks, axis):
    count = lax.axis_size(axis)
    rank = lax.axis_index(axis)
    doubled = jnp.concatenate([blocks, blocks], axis=0)
    slots = lax.dynamic_slice_in_dim(doubled, rank, count, 0)
    bit = 1
    while bit < count:
        chosen = [k for k in range(count) if k & bit]
        pairs = [(p, (p + bit) % count) for p in range(count)]
        arrived = lax.ppermute(slots[jnp.array(chosen)], axis, pairs)
        slots = slots.at[jnp.array(chosen)].set(arrived)
        bit *= 2
    doubled = jnp.concatenate([slots, slots], axis=0)
    return jnp.flip(lax.dynamic_slice_in_dim(doubled, rank + 1, count, 0), axis=0)


def twin_table(count, sign):
    low = 64 if count % 64 == 0 else count
    indices = jnp.arange(count, dtype=jnp.int32)
    low_ids = jnp.arange(low, dtype=jnp.int32)
    high_ids = jnp.arange(count // low, dtype=jnp.int32) * low
    low_ang = 2.0 * math.pi / count * (indices[:, None] * low_ids[None, :] % count).astype(jnp.float32)
    high_ang = 2.0 * math.pi / count * (indices[:, None] * high_ids[None, :] % count).astype(jnp.float32)
    low_cos, low_sin = jnp.cos(low_ang)[:, None, :], jnp.sin(low_ang)[:, None, :]
    high_cos, high_sin = jnp.cos(high_ang)[:, :, None], jnp.sin(high_ang)[:, :, None]
    cosine = (low_cos * high_cos - low_sin * high_sin).reshape(count, count)
    sine = (low_sin * high_cos + low_cos * high_sin).reshape(count, count)
    factor = 1.0 / math.sqrt(count)
    return (cosine * factor, sign * sine * factor)


def block_matrix(count, sign):
    cosine, sine_part = twin_table(count, sign)
    half = jnp.arange(2, dtype=jnp.int32)
    same = (half[:, None, None, None] == half[None, None, :, None])
    upper = half[:, None, None, None] == 0
    sine_signed = jnp.where(upper, sine_part[None, :, None, :], -sine_part[None, :, None, :])
    whole = jnp.where(same, cosine[None, :, None, :], sine_signed)
    return whole.reshape(2 * count, 2 * count)


def twist_leading(parts, freq_index, pos_index, seq_total, sign):
    product = (freq_index[:, None] * pos_index[None, :]).astype(jnp.float32)
    angles = 2.0 * math.pi / seq_total * product
    cosine = jnp.cos(angles)[None, :, :]
    sine_part = (sign * jnp.sin(angles))[None, :, :]
    real_part = parts[:, :, 0] * cosine - parts[:, :, 1] * sine_part
    imag_part = parts[:, :, 0] * sine_part + parts[:, :, 1] * cosine
    return jnp.stack([real_part, imag_part], axis=2)


def features(freq_index, seq_total):
    orders = 2 * jnp.arange(FEAT, dtype=jnp.int32) + 1
    product = freq_index[..., None] * orders % seq_total
    return jnp.cos(2.0 * math.pi / seq_total * product.astype(jnp.float32))


def feature_factors(inner, nblocks, seq_total):
    orders = 2 * jnp.arange(FEAT, dtype=jnp.int32) + 1
    inner_ids = jnp.arange(inner, dtype=jnp.int32)
    block_ids = jnp.arange(nblocks, dtype=jnp.int32)
    inner_prod = (inner_ids[:, None] * orders[None, :]) % inner
    block_prod = (block_ids[:, None] * orders[None, :]) % seq_total
    inner_ang = 2.0 * math.pi / inner * inner_prod.astype(jnp.float32)
    block_ang = 2.0 * math.pi / seq_total * block_prod.astype(jnp.float32)
    inner_tab = jnp.concatenate([jnp.cos(inner_ang), jnp.sin(inner_ang)], axis=1)
    return inner_tab, jnp.cos(block_ang), jnp.sin(block_ang)


def per_device(hidden_in, grad_out, norm_gain, skip_weight, filter_coef, run_lengths):
    local_tokens = hidden_in.shape[0]
    local_width = hidden_in.shape[1]
    seq_parts = lax.axis_size("seq")
    seq_rank = lax.axis_index("seq")
    seq_total = local_tokens * seq_parts
    nblocks = seq_total // BLOCK
    upcast = hidden_in.astype(jnp.float32)
    square_sums = taken_together(jnp.sum(upcast * upcast, axis=1), "ch")
    inverse_rms = lax.rsqrt(square_sums / D + epsilon)
    gain = norm_gain.astype(jnp.float32)
    normed = (upcast * inverse_rms[:, None] * gain[None, :]).astype(jnp.bfloat16)
    run_ends = jnp.cumsum(run_lengths)
    positions = seq_rank * local_tokens + jnp.arange(local_tokens, dtype=jnp.int32)
    run_index = jnp.sum((run_ends[None, :] <= positions[:, None]).astype(jnp.int32), axis=1)
    keep = run_index % 2 == 0
    gated = jnp.where(keep[:, None], grad_out, jnp.zeros_like(grad_out))
    forward_first = jnp.stack(twin_table(nblocks, -1.0), axis=2).astype(jnp.bfloat16)
    forward_second = block_matrix(BLOCK, -1.0).astype(jnp.bfloat16)
    back_first = block_matrix(BLOCK, 1.0).astype(jnp.bfloat16)
    cosine, sine_part = twin_table(nblocks, 1.0)
    back_second = jnp.stack([cosine, -sine_part], axis=1).astype(jnp.bfloat16)
    block_ids = jnp.arange(nblocks, dtype=jnp.int32)
    all_inner = jnp.arange(BLOCK, dtype=jnp.int32)
    width_share = local_width // seq_parts
    gated_moved = lax.all_to_all(gated.T, "seq", split_axis=0, concat_axis=1, tiled=True)
    gated_moved, normed = lax.optimization_barrier((gated_moved, normed))
    normed_moved = lax.all_to_all(normed.T, "seq", split_axis=0, concat_axis=1, tiled=True)
    moved = (normed_moved, gated_moved)
    coef_part = lax.dynamic_slice_in_dim(filter_coef, seq_rank * width_share, width_share, 2)

    def local_freq(field):
        blocks = field.reshape(width_share, nblocks, BLOCK)
        parts = jnp.einsum(
            "cnm,nkr->ckrm", blocks, forward_first, preferred_element_type=jnp.float32
        )
        turned = twist_leading(parts, block_ids, all_inner, seq_total, -1.0).astype(jnp.bfloat16)
        flat = turned.reshape(width_share, nblocks, 2 * BLOCK)
        spectrum = jnp.einsum(
            "ckm,mj->ckj", flat, forward_second, preferred_element_type=jnp.float32
        )
        return spectrum.reshape(width_share, nblocks, 2, BLOCK)

    spec_gated = local_freq(moved[1])
    inner_tab, block_cos, block_sin = feature_factors(BLOCK, nblocks, seq_total)
    coef_t = coef_part.astype(jnp.float32).transpose(2, 1, 0)[:, None, :, :]
    coef_mix = jnp.concatenate(
        [block_cos[None, :, None, :] * coef_t, -block_sin[None, :, None, :] * coef_t], axis=3
    )
    response = jnp.einsum(
        "ckrj,bj->ckrb", coef_mix, inner_tab,
        precision=lax.Precision.HIGHEST, preferred_element_type=jnp.float32,
    )
    prod_real = response[:, :, 0] * spec_gated[:, :, 0] + response[:, :, 1] * spec_gated[:, :, 1]
    prod_imag = response[:, :, 0] * spec_gated[:, :, 1] - response[:, :, 1] * spec_gated[:, :, 0]
    product = jnp.stack([prod_real, prod_imag], axis=2).astype(jnp.bfloat16)
    flat_product = product.reshape(width_share, nblocks, 2 * BLOCK)
    back_parts = jnp.einsum(
        "ckm,mj->ckj", flat_product, back_first, preferred_element_type=jnp.float32
    )
    back_parts = back_parts.reshape(width_share, nblocks, 2, BLOCK)
    back_twisted = twist_leading(back_parts, block_ids, all_inner, seq_total, 1.0).astype(
        jnp.bfloat16
    )
    time_field = jnp.einsum(
        "ckrm,krn->cnm", back_twisted, back_second, preferred_element_type=jnp.float32
    )
    time_field = time_field.reshape(width_share, seq_total).astype(jnp.bfloat16)
    time_field, normed_moved = lax.optimization_barrier((time_field, normed_moved))
    spec_normed = local_freq(normed_moved)
    grad_real = (
        spec_normed[:, :, 0] * spec_gated[:, :, 0] + spec_normed[:, :, 1] * spec_gated[:, :, 1]
    )
    grad_imag = (
        spec_normed[:, :, 0] * spec_gated[:, :, 1] - spec_normed[:, :, 1] * spec_gated[:, :, 0]
    )
    spec_grad = jnp.stack([grad_real, grad_imag], axis=2).astype(jnp.bfloat16)
    partial = jnp.einsum(
        "ckrb,bj->ckrj", spec_grad.astype(jnp.float32), inner_tab,
        precision=lax.Precision.HIGHEST, preferred_element_type=jnp.float32,
    )
    coef_local = jnp.sum(
        partial[..., :FEAT] * block_cos[None, :, None, :]
        - partial[..., FEAT:] * block_sin[None, :, None, :],
        axis=1,
    ).transpose(2, 1, 0)
    home_field = lax.all_to_all(time_field, "seq", split_axis=1, concat_axis=0, tiled=True)
    coef_rows = FEAT // seq_parts
    coef_blocks = coef_local.reshape(seq_parts, coef_rows, 2, width_share)
    coef_blocks = spread_blocks(coef_blocks, "seq")
    coef_sum = coef_blocks.transpose(1, 2, 0, 3).reshape(coef_rows, 2, local_width)
    filter_grad = coef_sum / math.sqrt(seq_total)
    conv_grad = home_field.T.astype(jnp.float32)
    normed_grad = conv_grad + skip_weight[None, :] * gated.astype(jnp.float32)
    scaled_grad = gain[None, :] * normed_grad
    row_dot = taken_together(jnp.sum(scaled_grad * upcast, axis=1), "ch")
    hidden_grad = (
        inverse_rms[:, None] * scaled_grad - upcast * (inverse_rms**3 * row_dot / D)[:, None]
    )
    return (hidden_grad.astype(jnp.bfloat16), filter_grad)


def solution(mesh):
    in_specs = (P("seq", "ch"), P("seq", "ch"), P("ch"), P("ch"), P(None, None, "ch"), P())
    out_specs = (P("seq", "ch"), P("seq", None, "ch"))
    return jax.shard_map(
        per_device, mesh=mesh, in_specs=in_specs, out_specs=out_specs, check_vma=False
    )
```

```python
import math

import jax
import jax.numpy as jnp
from jax import lax
from jax.sharding import PartitionSpec as P

D = 2048
BLOCK = 512
FEAT = 64


epsilon = 1e-06


def from_everyone(value, axis):
    copies = jnp.broadcast_to(value, (lax.axis_size(axis), *value.shape))
    return lax.all_to_all(copies, axis, split_axis=0, concat_axis=0, tiled=True)


def taken_together(value, axis):
    count = lax.axis_size(axis)
    step = 1
    while step < count:
        pairs = [(i, i ^ step) for i in range(count)]
        value = value + lax.ppermute(value, axis, pairs)
        step *= 2
    return value


def twin_table(count, sign):
    low = 64 if count % 64 == 0 else count
    indices = jnp.arange(count, dtype=jnp.int32)
    low_ids = jnp.arange(low, dtype=jnp.int32)
    high_ids = jnp.arange(count // low, dtype=jnp.int32) * low
    low_ang = 2.0 * math.pi / count * (indices[:, None] * low_ids[None, :] % count).astype(jnp.float32)
    high_ang = 2.0 * math.pi / count * (indices[:, None] * high_ids[None, :] % count).astype(jnp.float32)
    low_cos, low_sin = jnp.cos(low_ang)[:, None, :], jnp.sin(low_ang)[:, None, :]
    high_cos, high_sin = jnp.cos(high_ang)[:, :, None], jnp.sin(high_ang)[:, :, None]
    cosine = (low_cos * high_cos - low_sin * high_sin).reshape(count, count)
    sine = (low_sin * high_cos + low_cos * high_sin).reshape(count, count)
    factor = 1.0 / math.sqrt(count)
    return (cosine * factor, sign * sine * factor)


def block_matrix(count, sign):
    cosine, sine_part = twin_table(count, sign)
    half = jnp.arange(2, dtype=jnp.int32)
    same = (half[:, None, None, None] == half[None, None, :, None])
    upper = half[:, None, None, None] == 0
    sine_signed = jnp.where(upper, sine_part[None, :, None, :], -sine_part[None, :, None, :])
    whole = jnp.where(same, cosine[None, :, None, :], sine_signed)
    return whole.reshape(2 * count, 2 * count)


def twist_leading(parts, freq_index, pos_index, seq_total, sign):
    product = (freq_index[:, None] * pos_index[None, :]).astype(jnp.float32)
    angles = 2.0 * math.pi / seq_total * product
    cosine = jnp.cos(angles)[None, :, :]
    sine_part = (sign * jnp.sin(angles))[None, :, :]
    real_part = parts[:, :, 0] * cosine - parts[:, :, 1] * sine_part
    imag_part = parts[:, :, 0] * sine_part + parts[:, :, 1] * cosine
    return jnp.stack([real_part, imag_part], axis=2)


def features(freq_index, seq_total):
    orders = 2 * jnp.arange(FEAT, dtype=jnp.int32) + 1
    product = freq_index[..., None] * orders % seq_total
    return jnp.cos(2.0 * math.pi / seq_total * product.astype(jnp.float32))


def feature_factors(inner, nblocks, seq_total):
    orders = 2 * jnp.arange(FEAT, dtype=jnp.int32) + 1
    inner_ids = jnp.arange(inner, dtype=jnp.int32)
    block_ids = jnp.arange(nblocks, dtype=jnp.int32)
    inner_prod = (inner_ids[:, None] * orders[None, :]) % inner
    block_prod = (block_ids[:, None] * orders[None, :]) % seq_total
    inner_ang = 2.0 * math.pi / inner * inner_prod.astype(jnp.float32)
    block_ang = 2.0 * math.pi / seq_total * block_prod.astype(jnp.float32)
    inner_tab = jnp.concatenate([jnp.cos(inner_ang), jnp.sin(inner_ang)], axis=1)
    return inner_tab, jnp.cos(block_ang), jnp.sin(block_ang)


def per_device(hidden_in, grad_out, norm_gain, skip_weight, filter_coef, run_lengths):
    local_tokens = hidden_in.shape[0]
    local_width = hidden_in.shape[1]
    seq_parts = lax.axis_size("seq")
    seq_rank = lax.axis_index("seq")
    seq_total = local_tokens * seq_parts
    nblocks = seq_total // BLOCK
    upcast = hidden_in.astype(jnp.float32)
    square_sums = taken_together(jnp.sum(upcast * upcast, axis=1), "ch")
    inverse_rms = lax.rsqrt(square_sums / D + epsilon)
    gain = norm_gain.astype(jnp.float32)
    normed = (upcast * inverse_rms[:, None] * gain[None, :]).astype(jnp.bfloat16)
    run_ends = jnp.cumsum(run_lengths)
    positions = seq_rank * local_tokens + jnp.arange(local_tokens, dtype=jnp.int32)
    run_index = jnp.sum((run_ends[None, :] <= positions[:, None]).astype(jnp.int32), axis=1)
    keep = run_index % 2 == 0
    gated = jnp.where(keep[:, None], grad_out, jnp.zeros_like(grad_out))
    forward_first = jnp.stack(twin_table(nblocks, -1.0), axis=2).astype(jnp.bfloat16)
    forward_second = block_matrix(BLOCK, -1.0).astype(jnp.bfloat16)
    back_first = block_matrix(BLOCK, 1.0).astype(jnp.bfloat16)
    cosine, sine_part = twin_table(nblocks, 1.0)
    back_second = jnp.stack([cosine, -sine_part], axis=1).astype(jnp.bfloat16)
    block_ids = jnp.arange(nblocks, dtype=jnp.int32)
    all_inner = jnp.arange(BLOCK, dtype=jnp.int32)
    width_share = local_width // seq_parts
    gated, inverse_rms = lax.optimization_barrier((gated, inverse_rms))
    gated_moved = lax.all_to_all(gated.T, "seq", split_axis=0, concat_axis=1, tiled=True)
    gated_moved, normed = lax.optimization_barrier((gated_moved, normed))
    normed_moved = lax.all_to_all(normed.T, "seq", split_axis=0, concat_axis=1, tiled=True)
    moved = (normed_moved, gated_moved)
    coef_part = lax.dynamic_slice_in_dim(filter_coef, seq_rank * width_share, width_share, 2)

    def local_freq(field):
        blocks = field.reshape(width_share, nblocks, BLOCK)
        parts = jnp.einsum(
            "cnm,nkr->ckrm", blocks, forward_first, preferred_element_type=jnp.float32
        )
        turned = twist_leading(parts, block_ids, all_inner, seq_total, -1.0).astype(jnp.bfloat16)
        flat = turned.reshape(width_share, nblocks, 2 * BLOCK)
        spectrum = jnp.einsum(
            "ckm,mj->ckj", flat, forward_second, preferred_element_type=jnp.float32
        )
        return spectrum.reshape(width_share, nblocks, 2, BLOCK)

    spec_gated = local_freq(moved[1])
    inner_tab, block_cos, block_sin = feature_factors(BLOCK, nblocks, seq_total)
    coef_t = coef_part.astype(jnp.float32).transpose(2, 1, 0)[:, None, :, :]
    coef_mix = jnp.concatenate(
        [block_cos[None, :, None, :] * coef_t, -block_sin[None, :, None, :] * coef_t], axis=3
    )
    response = jnp.einsum(
        "ckrj,bj->ckrb", coef_mix, inner_tab,
        precision=lax.Precision.HIGHEST, preferred_element_type=jnp.float32,
    )
    prod_real = response[:, :, 0] * spec_gated[:, :, 0] + response[:, :, 1] * spec_gated[:, :, 1]
    prod_imag = response[:, :, 0] * spec_gated[:, :, 1] - response[:, :, 1] * spec_gated[:, :, 0]
    product = jnp.stack([prod_real, prod_imag], axis=2).astype(jnp.bfloat16)
    flat_product = product.reshape(width_share, nblocks, 2 * BLOCK)
    back_parts = jnp.einsum(
        "ckm,mj->ckj", flat_product, back_first, preferred_element_type=jnp.float32
    )
    back_parts = back_parts.reshape(width_share, nblocks, 2, BLOCK)
    back_twisted = twist_leading(back_parts, block_ids, all_inner, seq_total, 1.0).astype(
        jnp.bfloat16
    )
    time_field = jnp.einsum(
        "ckrm,krn->cnm", back_twisted, back_second, preferred_element_type=jnp.float32
    )
    time_field = time_field.reshape(width_share, seq_total).astype(jnp.bfloat16)
    time_field, normed_moved = lax.optimization_barrier((time_field, normed_moved))
    spec_normed = local_freq(normed_moved)
    grad_real = (
        spec_normed[:, :, 0] * spec_gated[:, :, 0] + spec_normed[:, :, 1] * spec_gated[:, :, 1]
    )
    grad_imag = (
        spec_normed[:, :, 0] * spec_gated[:, :, 1] - spec_normed[:, :, 1] * spec_gated[:, :, 0]
    )
    spec_grad = jnp.stack([grad_real, grad_imag], axis=2).astype(jnp.bfloat16)
    partial = jnp.einsum(
        "ckrb,bj->ckrj", spec_grad.astype(jnp.float32), inner_tab,
        precision=lax.Precision.HIGHEST, preferred_element_type=jnp.float32,
    )
    coef_local = jnp.sum(
        partial[..., :FEAT] * block_cos[None, :, None, :]
        - partial[..., FEAT:] * block_sin[None, :, None, :],
        axis=1,
    ).transpose(2, 1, 0)
    home_field = lax.all_to_all(time_field, "seq", split_axis=1, concat_axis=0, tiled=True)
    coef_local, home_field = lax.optimization_barrier((coef_local, home_field))
    coef_sum = lax.all_to_all(coef_local, "seq", split_axis=0, concat_axis=2, tiled=True)
    filter_grad = coef_sum / math.sqrt(seq_total)
    conv_grad = home_field.T.astype(jnp.float32)
    normed_grad = conv_grad + skip_weight[None, :] * gated.astype(jnp.float32)
    scaled_grad = gain[None, :] * normed_grad
    row_dot = taken_together(jnp.sum(scaled_grad * upcast, axis=1), "ch")
    hidden_grad = (
        inverse_rms[:, None] * scaled_grad - upcast * (inverse_rms**3 * row_dot / D)[:, None]
    )
    return (hidden_grad.astype(jnp.bfloat16), filter_grad)


def solution(mesh):
    in_specs = (P("seq", "ch"), P("seq", "ch"), P("ch"), P("ch"), P(None, None, "ch"), P())
    out_specs = (P("seq", "ch"), P("seq", None, "ch"))
    return jax.shard_map(
        per_device, mesh=mesh, in_specs=in_specs, out_specs=out_specs, check_vma=False
    )
```

```python
import math

import jax
import jax.numpy as jnp
from jax import lax
from jax.sharding import PartitionSpec as P

D = 2048
BLOCK = 512
FEAT = 64


epsilon = 1e-06


def from_everyone(value, axis):
    copies = jnp.broadcast_to(value, (lax.axis_size(axis), *value.shape))
    return lax.all_to_all(copies, axis, split_axis=0, concat_axis=0, tiled=True)


def taken_together(value, axis):
    count = lax.axis_size(axis)
    step = 1
    while step < count:
        pairs = [(i, i ^ step) for i in range(count)]
        value = value + lax.ppermute(value, axis, pairs)
        step *= 2
    return value


def twin_table(count, sign):
    low = 64 if count % 64 == 0 else count
    indices = jnp.arange(count, dtype=jnp.int32)
    low_ids = jnp.arange(low, dtype=jnp.int32)
    high_ids = jnp.arange(count // low, dtype=jnp.int32) * low
    low_ang = 2.0 * math.pi / count * (indices[:, None] * low_ids[None, :] % count).astype(jnp.float32)
    high_ang = 2.0 * math.pi / count * (indices[:, None] * high_ids[None, :] % count).astype(jnp.float32)
    low_cos, low_sin = jnp.cos(low_ang)[:, None, :], jnp.sin(low_ang)[:, None, :]
    high_cos, high_sin = jnp.cos(high_ang)[:, :, None], jnp.sin(high_ang)[:, :, None]
    cosine = (low_cos * high_cos - low_sin * high_sin).reshape(count, count)
    sine = (low_sin * high_cos + low_cos * high_sin).reshape(count, count)
    factor = 1.0 / math.sqrt(count)
    return (cosine * factor, sign * sine * factor)


def block_matrix(count, sign):
    cosine, sine_part = twin_table(count, sign)
    half = jnp.arange(2, dtype=jnp.int32)
    same = (half[:, None, None, None] == half[None, None, :, None])
    upper = half[:, None, None, None] == 0
    sine_signed = jnp.where(upper, sine_part[None, :, None, :], -sine_part[None, :, None, :])
    whole = jnp.where(same, cosine[None, :, None, :], sine_signed)
    return whole.reshape(2 * count, 2 * count)


def twist_leading(parts, freq_index, pos_index, seq_total, sign):
    product = (freq_index[:, None] * pos_index[None, :]).astype(jnp.float32)
    angles = 2.0 * math.pi / seq_total * product
    cosine = jnp.cos(angles)[None, :, :]
    sine_part = (sign * jnp.sin(angles))[None, :, :]
    real_part = parts[:, :, 0] * cosine - parts[:, :, 1] * sine_part
    imag_part = parts[:, :, 0] * sine_part + parts[:, :, 1] * cosine
    return jnp.stack([real_part, imag_part], axis=2)


def features(freq_index, seq_total):
    orders = 2 * jnp.arange(FEAT, dtype=jnp.int32) + 1
    product = freq_index[..., None] * orders % seq_total
    return jnp.cos(2.0 * math.pi / seq_total * product.astype(jnp.float32))


def feature_factors(inner, nblocks, seq_total):
    orders = 2 * jnp.arange(FEAT, dtype=jnp.int32) + 1
    inner_ids = jnp.arange(inner, dtype=jnp.int32)
    block_ids = jnp.arange(nblocks, dtype=jnp.int32)
    inner_prod = (inner_ids[:, None] * orders[None, :]) % inner
    block_prod = (block_ids[:, None] * orders[None, :]) % seq_total
    inner_ang = 2.0 * math.pi / inner * inner_prod.astype(jnp.float32)
    block_ang = 2.0 * math.pi / seq_total * block_prod.astype(jnp.float32)
    inner_tab = jnp.concatenate([jnp.cos(inner_ang), jnp.sin(inner_ang)], axis=1)
    return inner_tab, jnp.cos(block_ang), jnp.sin(block_ang)


def per_device(hidden_in, grad_out, norm_gain, skip_weight, filter_coef, run_lengths):
    local_tokens = hidden_in.shape[0]
    local_width = hidden_in.shape[1]
    seq_parts = lax.axis_size("seq")
    seq_rank = lax.axis_index("seq")
    seq_total = local_tokens * seq_parts
    nblocks = seq_total // BLOCK
    upcast = hidden_in.astype(jnp.float32)
    square_sums = taken_together(jnp.sum(upcast * upcast, axis=1), "ch")
    inverse_rms = lax.rsqrt(square_sums / D + epsilon)
    gain = norm_gain.astype(jnp.float32)
    normed = (upcast * inverse_rms[:, None] * gain[None, :]).astype(jnp.bfloat16)
    run_ends = jnp.cumsum(run_lengths)
    positions = seq_rank * local_tokens + jnp.arange(local_tokens, dtype=jnp.int32)
    run_index = jnp.sum((run_ends[None, :] <= positions[:, None]).astype(jnp.int32), axis=1)
    keep = run_index % 2 == 0
    gated = jnp.where(keep[:, None], grad_out, jnp.zeros_like(grad_out))
    forward_first = jnp.stack(twin_table(nblocks, -1.0), axis=2).astype(jnp.bfloat16)
    forward_second = block_matrix(BLOCK, -1.0).astype(jnp.bfloat16)
    cosine, sine_part = twin_table(nblocks, 1.0)
    back_second = jnp.stack([cosine, -sine_part], axis=1).astype(jnp.bfloat16)
    block_ids = jnp.arange(nblocks, dtype=jnp.int32)
    all_inner = jnp.arange(BLOCK, dtype=jnp.int32)
    width_share = local_width // seq_parts
    gated, inverse_rms = lax.optimization_barrier((gated, inverse_rms))
    gated_moved = lax.all_to_all(gated.T, "seq", split_axis=0, concat_axis=1, tiled=True)
    gated_moved, normed = lax.optimization_barrier((gated_moved, normed))
    normed_moved = lax.all_to_all(normed.T, "seq", split_axis=0, concat_axis=1, tiled=True)
    moved = (normed_moved, gated_moved)
    coef_part = lax.dynamic_slice_in_dim(filter_coef, seq_rank * width_share, width_share, 2)

    def local_freq(field):
        blocks = field.reshape(width_share, nblocks, BLOCK)
        parts = jnp.einsum(
            "cnm,nkr->ckrm", blocks, forward_first, preferred_element_type=jnp.float32
        )
        turned = twist_leading(parts, block_ids, all_inner, seq_total, -1.0).astype(jnp.bfloat16)
        flat = turned.reshape(width_share, nblocks, 2 * BLOCK)
        spectrum = jnp.einsum(
            "ckm,mj->ckj", flat, forward_second, preferred_element_type=jnp.float32
        )
        return spectrum.reshape(width_share, nblocks, 2, BLOCK)

    spec_gated = local_freq(moved[1])
    inner_tab, block_cos, block_sin = feature_factors(BLOCK, nblocks, seq_total)
    coef_t = coef_part.astype(jnp.float32).transpose(2, 1, 0)[:, None, :, :]
    coef_mix = jnp.concatenate(
        [block_cos[None, :, None, :] * coef_t, -block_sin[None, :, None, :] * coef_t], axis=3
    )
    response = jnp.einsum(
        "ckrj,bj->ckrb", coef_mix, inner_tab,
        precision=lax.Precision.HIGHEST, preferred_element_type=jnp.float32,
    )
    prod_real = response[:, :, 0] * spec_gated[:, :, 0] + response[:, :, 1] * spec_gated[:, :, 1]
    prod_imag = response[:, :, 0] * spec_gated[:, :, 1] - response[:, :, 1] * spec_gated[:, :, 0]
    product = jnp.stack([prod_real, prod_imag], axis=2).astype(jnp.bfloat16)
    flat_product = product.reshape(width_share, nblocks, 2 * BLOCK)
    back_parts = jnp.einsum(
        "ckm,jm->ckj", flat_product, forward_second, preferred_element_type=jnp.float32
    )
    back_parts = back_parts.reshape(width_share, nblocks, 2, BLOCK)
    back_twisted = twist_leading(back_parts, block_ids, all_inner, seq_total, 1.0).astype(
        jnp.bfloat16
    )
    time_field = jnp.einsum(
        "ckrm,krn->cnm", back_twisted, back_second, preferred_element_type=jnp.float32
    )
    time_field = time_field.reshape(width_share, seq_total).astype(jnp.bfloat16)
    time_field, normed_moved = lax.optimization_barrier((time_field, normed_moved))
    spec_normed = local_freq(normed_moved)
    grad_real = (
        spec_normed[:, :, 0] * spec_gated[:, :, 0] + spec_normed[:, :, 1] * spec_gated[:, :, 1]
    )
    grad_imag = (
        spec_normed[:, :, 0] * spec_gated[:, :, 1] - spec_normed[:, :, 1] * spec_gated[:, :, 0]
    )
    spec_grad = jnp.stack([grad_real, grad_imag], axis=2).astype(jnp.bfloat16)
    partial = jnp.einsum(
        "ckrb,bj->ckrj", spec_grad.astype(jnp.float32), inner_tab,
        precision=lax.Precision.HIGHEST, preferred_element_type=jnp.float32,
    )
    coef_local = jnp.sum(
        partial[..., :FEAT] * block_cos[None, :, None, :]
        - partial[..., FEAT:] * block_sin[None, :, None, :],
        axis=1,
    ).transpose(2, 1, 0)
    home_field = lax.all_to_all(time_field, "seq", split_axis=1, concat_axis=0, tiled=True)
    coef_local, home_field = lax.optimization_barrier((coef_local, home_field))
    coef_sum = lax.all_to_all(coef_local, "seq", split_axis=0, concat_axis=2, tiled=True)
    filter_grad = coef_sum / math.sqrt(seq_total)
    conv_grad = home_field.T.astype(jnp.float32)
    normed_grad = conv_grad + skip_weight[None, :] * gated.astype(jnp.float32)
    scaled_grad = gain[None, :] * normed_grad
    row_dot = taken_together(jnp.sum(scaled_grad * upcast, axis=1), "ch")
    hidden_grad = (
        inverse_rms[:, None] * scaled_grad - upcast * (inverse_rms**3 * row_dot / D)[:, None]
    )
    return (hidden_grad.astype(jnp.bfloat16), filter_grad)


def solution(mesh):
    in_specs = (P("seq", "ch"), P("seq", "ch"), P("ch"), P("ch"), P(None, None, "ch"), P())
    out_specs = (P("seq", "ch"), P("seq", None, "ch"))
    return jax.shard_map(
        per_device, mesh=mesh, in_specs=in_specs, out_specs=out_specs, check_vma=False
    )
```

```python
import math

import jax
import jax.numpy as jnp
from jax import lax
from jax.sharding import PartitionSpec as P

D = 2048
BLOCK = 512
FEAT = 64


epsilon = 1e-06


def from_everyone(value, axis):
    copies = jnp.broadcast_to(value, (lax.axis_size(axis), *value.shape))
    return lax.all_to_all(copies, axis, split_axis=0, concat_axis=0, tiled=True)


def taken_together(value, axis):
    count = lax.axis_size(axis)
    step = count // 2
    while step >= 1:
        pairs = [(i, i ^ step) for i in range(count)]
        value = value + lax.ppermute(value, axis, pairs)
        step //= 2
    return value


def twin_table(count, sign):
    low = 64 if count % 64 == 0 else count
    indices = jnp.arange(count, dtype=jnp.int32)
    low_ids = jnp.arange(low, dtype=jnp.int32)
    high_ids = jnp.arange(count // low, dtype=jnp.int32) * low
    low_ang = 2.0 * math.pi / count * (indices[:, None] * low_ids[None, :] % count).astype(jnp.float32)
    high_ang = 2.0 * math.pi / count * (indices[:, None] * high_ids[None, :] % count).astype(jnp.float32)
    low_cos, low_sin = jnp.cos(low_ang)[:, None, :], jnp.sin(low_ang)[:, None, :]
    high_cos, high_sin = jnp.cos(high_ang)[:, :, None], jnp.sin(high_ang)[:, :, None]
    cosine = (low_cos * high_cos - low_sin * high_sin).reshape(count, count)
    sine = (low_sin * high_cos + low_cos * high_sin).reshape(count, count)
    factor = 1.0 / math.sqrt(count)
    return (cosine * factor, sign * sine * factor)


def block_matrix(count, sign):
    cosine, sine_part = twin_table(count, sign)
    half = jnp.arange(2, dtype=jnp.int32)
    same = (half[:, None, None, None] == half[None, None, :, None])
    upper = half[:, None, None, None] == 0
    sine_signed = jnp.where(upper, sine_part[None, :, None, :], -sine_part[None, :, None, :])
    whole = jnp.where(same, cosine[None, :, None, :], sine_signed)
    return whole.reshape(2 * count, 2 * count)


def twist_leading(parts, freq_index, pos_index, seq_total, sign):
    product = (freq_index[:, None] * pos_index[None, :]).astype(jnp.float32)
    angles = 2.0 * math.pi / seq_total * product
    cosine = jnp.cos(angles)[None, :, :]
    sine_part = (sign * jnp.sin(angles))[None, :, :]
    real_part = parts[:, :, 0] * cosine - parts[:, :, 1] * sine_part
    imag_part = parts[:, :, 0] * sine_part + parts[:, :, 1] * cosine
    return jnp.stack([real_part, imag_part], axis=2)


def features(freq_index, seq_total):
    orders = 2 * jnp.arange(FEAT, dtype=jnp.int32) + 1
    product = freq_index[..., None] * orders % seq_total
    return jnp.cos(2.0 * math.pi / seq_total * product.astype(jnp.float32))


def feature_factors(inner, nblocks, seq_total):
    orders = 2 * jnp.arange(FEAT, dtype=jnp.int32) + 1
    inner_ids = jnp.arange(inner, dtype=jnp.int32)
    block_ids = jnp.arange(nblocks, dtype=jnp.int32)
    inner_prod = (inner_ids[:, None] * orders[None, :]) % inner
    block_prod = (block_ids[:, None] * orders[None, :]) % seq_total
    inner_ang = 2.0 * math.pi / inner * inner_prod.astype(jnp.float32)
    block_ang = 2.0 * math.pi / seq_total * block_prod.astype(jnp.float32)
    inner_tab = jnp.concatenate([jnp.cos(inner_ang), jnp.sin(inner_ang)], axis=1)
    return inner_tab, jnp.cos(block_ang), jnp.sin(block_ang)


def per_device(hidden_in, grad_out, norm_gain, skip_weight, filter_coef, run_lengths):
    local_tokens = hidden_in.shape[0]
    local_width = hidden_in.shape[1]
    seq_parts = lax.axis_size("seq")
    seq_rank = lax.axis_index("seq")
    seq_total = local_tokens * seq_parts
    nblocks = seq_total // BLOCK
    upcast = hidden_in.astype(jnp.float32)
    square_sums = taken_together(jnp.sum(upcast * upcast, axis=1), "ch")
    inverse_rms = lax.rsqrt(square_sums / D + epsilon)
    gain = norm_gain.astype(jnp.float32)
    normed = (upcast * inverse_rms[:, None] * gain[None, :]).astype(jnp.bfloat16)
    run_ends = jnp.cumsum(run_lengths)
    positions = seq_rank * local_tokens + jnp.arange(local_tokens, dtype=jnp.int32)
    run_index = jnp.sum((run_ends[None, :] <= positions[:, None]).astype(jnp.int32), axis=1)
    keep = run_index % 2 == 0
    gated = jnp.where(keep[:, None], grad_out, jnp.zeros_like(grad_out))
    forward_first = jnp.stack(twin_table(nblocks, -1.0), axis=2).astype(jnp.bfloat16)
    forward_second = block_matrix(BLOCK, -1.0).astype(jnp.bfloat16)
    back_first = block_matrix(BLOCK, 1.0).astype(jnp.bfloat16)
    cosine, sine_part = twin_table(nblocks, 1.0)
    back_second = jnp.stack([cosine, -sine_part], axis=1).astype(jnp.bfloat16)
    block_ids = jnp.arange(nblocks, dtype=jnp.int32)
    all_inner = jnp.arange(BLOCK, dtype=jnp.int32)
    width_share = local_width // seq_parts
    gated, inverse_rms = lax.optimization_barrier((gated, inverse_rms))
    gated_moved = lax.all_to_all(gated.T, "seq", split_axis=0, concat_axis=1, tiled=True)
    gated_moved, normed = lax.optimization_barrier((gated_moved, normed))
    normed_moved = lax.all_to_all(normed.T, "seq", split_axis=0, concat_axis=1, tiled=True)
    moved = (normed_moved, gated_moved)
    coef_part = lax.dynamic_slice_in_dim(filter_coef, seq_rank * width_share, width_share, 2)

    def local_freq(field):
        blocks = field.reshape(width_share, nblocks, BLOCK)
        parts = jnp.einsum(
            "cnm,nkr->ckrm", blocks, forward_first, preferred_element_type=jnp.float32
        )
        turned = twist_leading(parts, block_ids, all_inner, seq_total, -1.0).astype(jnp.bfloat16)
        flat = turned.reshape(width_share, nblocks, 2 * BLOCK)
        spectrum = jnp.einsum(
            "ckm,mj->ckj", flat, forward_second, preferred_element_type=jnp.float32
        )
        return spectrum.reshape(width_share, nblocks, 2, BLOCK)

    spec_gated = local_freq(moved[1])
    inner_tab, block_cos, block_sin = feature_factors(BLOCK, nblocks, seq_total)
    coef_t = coef_part.astype(jnp.float32).transpose(2, 1, 0)[:, None, :, :]
    coef_mix = jnp.concatenate(
        [block_cos[None, :, None, :] * coef_t, -block_sin[None, :, None, :] * coef_t], axis=3
    )
    response = jnp.einsum(
        "ckrj,bj->ckrb", coef_mix, inner_tab,
        precision=lax.Precision.HIGHEST, preferred_element_type=jnp.float32,
    )
    prod_real = response[:, :, 0] * spec_gated[:, :, 0] + response[:, :, 1] * spec_gated[:, :, 1]
    prod_imag = response[:, :, 0] * spec_gated[:, :, 1] - response[:, :, 1] * spec_gated[:, :, 0]
    product = jnp.stack([prod_real, prod_imag], axis=2).astype(jnp.bfloat16)
    flat_product = product.reshape(width_share, nblocks, 2 * BLOCK)
    back_parts = jnp.einsum(
        "ckm,mj->ckj", flat_product, back_first, preferred_element_type=jnp.float32
    )
    back_parts = back_parts.reshape(width_share, nblocks, 2, BLOCK)
    back_twisted = twist_leading(back_parts, block_ids, all_inner, seq_total, 1.0).astype(
        jnp.bfloat16
    )
    time_field = jnp.einsum(
        "ckrm,krn->cnm", back_twisted, back_second, preferred_element_type=jnp.float32
    )
    time_field = time_field.reshape(width_share, seq_total).astype(jnp.bfloat16)
    time_field, normed_moved = lax.optimization_barrier((time_field, normed_moved))
    spec_normed = local_freq(normed_moved)
    grad_real = (
        spec_normed[:, :, 0] * spec_gated[:, :, 0] + spec_normed[:, :, 1] * spec_gated[:, :, 1]
    )
    grad_imag = (
        spec_normed[:, :, 0] * spec_gated[:, :, 1] - spec_normed[:, :, 1] * spec_gated[:, :, 0]
    )
    spec_grad = jnp.stack([grad_real, grad_imag], axis=2).astype(jnp.bfloat16)
    partial = jnp.einsum(
        "ckrb,bj->ckrj", spec_grad.astype(jnp.float32), inner_tab,
        precision=lax.Precision.HIGHEST, preferred_element_type=jnp.float32,
    )
    coef_local = jnp.sum(
        partial[..., :FEAT] * block_cos[None, :, None, :]
        - partial[..., FEAT:] * block_sin[None, :, None, :],
        axis=1,
    ).transpose(2, 1, 0)
    home_field = lax.all_to_all(time_field, "seq", split_axis=1, concat_axis=0, tiled=True)
    coef_local, home_field = lax.optimization_barrier((coef_local, home_field))
    coef_sum = lax.all_to_all(coef_local, "seq", split_axis=0, concat_axis=2, tiled=True)
    filter_grad = coef_sum / math.sqrt(seq_total)
    conv_grad = home_field.T.astype(jnp.float32)
    normed_grad = conv_grad + skip_weight[None, :] * gated.astype(jnp.float32)
    scaled_grad = gain[None, :] * normed_grad
    row_dot = taken_together(jnp.sum(scaled_grad * upcast, axis=1), "ch")
    hidden_grad = (
        inverse_rms[:, None] * scaled_grad - upcast * (inverse_rms**3 * row_dot / D)[:, None]
    )
    return (hidden_grad.astype(jnp.bfloat16), filter_grad)


def solution(mesh):
    in_specs = (P("seq", "ch"), P("seq", "ch"), P("ch"), P("ch"), P(None, None, "ch"), P())
    out_specs = (P("seq", "ch"), P("seq", None, "ch"))
    return jax.shard_map(
        per_device, mesh=mesh, in_specs=in_specs, out_specs=out_specs, check_vma=False
    )
```

```python
import math

import jax
import jax.numpy as jnp
from jax import lax
from jax.sharding import PartitionSpec as P

D = 2048
BLOCK = 512
FEAT = 64


epsilon = 1e-06


def from_everyone(value, axis):
    copies = jnp.broadcast_to(value, (lax.axis_size(axis), *value.shape))
    return lax.all_to_all(copies, axis, split_axis=0, concat_axis=0, tiled=True)


def taken_together(value, axis):
    count = lax.axis_size(axis)
    step = 1
    while step < count:
        pairs = [(i, i ^ step) for i in range(count)]
        value = value + lax.ppermute(value, axis, pairs)
        step *= 2
    return value


def twin_table(count, sign):
    low = 64 if count % 64 == 0 else count
    indices = jnp.arange(count, dtype=jnp.int32)
    low_ids = jnp.arange(low, dtype=jnp.int32)
    high_ids = jnp.arange(count // low, dtype=jnp.int32) * low
    low_ang = 2.0 * math.pi / count * (indices[:, None] * low_ids[None, :] % count).astype(jnp.float32)
    high_ang = 2.0 * math.pi / count * (indices[:, None] * high_ids[None, :] % count).astype(jnp.float32)
    low_cos, low_sin = jnp.cos(low_ang)[:, None, :], jnp.sin(low_ang)[:, None, :]
    high_cos, high_sin = jnp.cos(high_ang)[:, :, None], jnp.sin(high_ang)[:, :, None]
    cosine = (low_cos * high_cos - low_sin * high_sin).reshape(count, count)
    sine = (low_sin * high_cos + low_cos * high_sin).reshape(count, count)
    factor = 1.0 / math.sqrt(count)
    return (cosine * factor, sign * sine * factor)


def block_matrix(count, sign):
    cosine, sine_part = twin_table(count, sign)
    half = jnp.arange(2, dtype=jnp.int32)
    same = (half[:, None, None, None] == half[None, None, :, None])
    upper = half[:, None, None, None] == 0
    sine_signed = jnp.where(upper, sine_part[None, :, None, :], -sine_part[None, :, None, :])
    return jnp.where(same, cosine[None, :, None, :], sine_signed)


def twist_leading(parts, freq_index, pos_index, seq_total, sign):
    product = (freq_index[:, None] * pos_index[None, :]).astype(jnp.float32)
    angles = 2.0 * math.pi / seq_total * product
    cosine = jnp.cos(angles)[None, :, :]
    sine_part = (sign * jnp.sin(angles))[None, :, :]
    real_part = parts[:, :, 0] * cosine - parts[:, :, 1] * sine_part
    imag_part = parts[:, :, 0] * sine_part + parts[:, :, 1] * cosine
    return jnp.stack([real_part, imag_part], axis=2)


def features(freq_index, seq_total):
    orders = 2 * jnp.arange(FEAT, dtype=jnp.int32) + 1
    product = freq_index[..., None] * orders % seq_total
    return jnp.cos(2.0 * math.pi / seq_total * product.astype(jnp.float32))


def feature_factors(inner, nblocks, seq_total):
    orders = 2 * jnp.arange(FEAT, dtype=jnp.int32) + 1
    inner_ids = jnp.arange(inner, dtype=jnp.int32)
    block_ids = jnp.arange(nblocks, dtype=jnp.int32)
    inner_prod = (inner_ids[:, None] * orders[None, :]) % inner
    block_prod = (block_ids[:, None] * orders[None, :]) % seq_total
    inner_ang = 2.0 * math.pi / inner * inner_prod.astype(jnp.float32)
    block_ang = 2.0 * math.pi / seq_total * block_prod.astype(jnp.float32)
    inner_tab = jnp.concatenate([jnp.cos(inner_ang), jnp.sin(inner_ang)], axis=1)
    return inner_tab, jnp.cos(block_ang), jnp.sin(block_ang)


def per_device(hidden_in, grad_out, norm_gain, skip_weight, filter_coef, run_lengths):
    local_tokens = hidden_in.shape[0]
    local_width = hidden_in.shape[1]
    seq_parts = lax.axis_size("seq")
    seq_rank = lax.axis_index("seq")
    seq_total = local_tokens * seq_parts
    nblocks = seq_total // BLOCK
    upcast = hidden_in.astype(jnp.float32)
    square_sums = taken_together(jnp.sum(upcast * upcast, axis=1), "ch")
    inverse_rms = lax.rsqrt(square_sums / D + epsilon)
    gain = norm_gain.astype(jnp.float32)
    normed = (upcast * inverse_rms[:, None] * gain[None, :]).astype(jnp.bfloat16)
    run_ends = jnp.cumsum(run_lengths)
    positions = seq_rank * local_tokens + jnp.arange(local_tokens, dtype=jnp.int32)
    run_index = jnp.sum((run_ends[None, :] <= positions[:, None]).astype(jnp.int32), axis=1)
    keep = run_index % 2 == 0
    gated = jnp.where(keep[:, None], grad_out, jnp.zeros_like(grad_out))
    forward_first = jnp.stack(twin_table(nblocks, -1.0), axis=2).astype(jnp.bfloat16)
    forward_second = block_matrix(BLOCK, -1.0).astype(jnp.bfloat16)
    back_first = block_matrix(BLOCK, 1.0).astype(jnp.bfloat16)
    cosine, sine_part = twin_table(nblocks, 1.0)
    back_second = jnp.stack([cosine, -sine_part], axis=1).astype(jnp.bfloat16)
    block_ids = jnp.arange(nblocks, dtype=jnp.int32)
    all_inner = jnp.arange(BLOCK, dtype=jnp.int32)
    width_share = local_width // seq_parts
    gated, inverse_rms = lax.optimization_barrier((gated, inverse_rms))
    gated_moved = lax.all_to_all(gated.T, "seq", split_axis=0, concat_axis=1, tiled=True)
    gated_moved, normed = lax.optimization_barrier((gated_moved, normed))
    normed_moved = lax.all_to_all(normed.T, "seq", split_axis=0, concat_axis=1, tiled=True)
    moved = (normed_moved, gated_moved)
    coef_part = lax.dynamic_slice_in_dim(filter_coef, seq_rank * width_share, width_share, 2)

    def local_freq(field):
        blocks = field.reshape(width_share, nblocks, BLOCK)
        parts = jnp.einsum(
            "cnm,nkr->ckrm", blocks, forward_first, preferred_element_type=jnp.float32
        )
        turned = twist_leading(parts, block_ids, all_inner, seq_total, -1.0).astype(jnp.bfloat16)
        return jnp.einsum(
            "ckrm,rmsj->cksj", turned, forward_second, preferred_element_type=jnp.float32
        )

    spec_gated = local_freq(moved[1])
    inner_tab, block_cos, block_sin = feature_factors(BLOCK, nblocks, seq_total)
    coef_t = coef_part.astype(jnp.float32).transpose(2, 1, 0)[:, None, :, :]
    coef_mix = jnp.concatenate(
        [block_cos[None, :, None, :] * coef_t, -block_sin[None, :, None, :] * coef_t], axis=3
    )
    response = jnp.einsum(
        "ckrj,bj->ckrb", coef_mix, inner_tab,
        precision=lax.Precision.HIGHEST, preferred_element_type=jnp.float32,
    )
    prod_real = response[:, :, 0] * spec_gated[:, :, 0] + response[:, :, 1] * spec_gated[:, :, 1]
    prod_imag = response[:, :, 0] * spec_gated[:, :, 1] - response[:, :, 1] * spec_gated[:, :, 0]
    product = jnp.stack([prod_real, prod_imag], axis=2).astype(jnp.bfloat16)
    back_parts = jnp.einsum(
        "ckrm,rmsj->cksj", product, back_first, preferred_element_type=jnp.float32
    )
    back_twisted = twist_leading(back_parts, block_ids, all_inner, seq_total, 1.0).astype(
        jnp.bfloat16
    )
    time_field = jnp.einsum(
        "ckrm,krn->cnm", back_twisted, back_second, preferred_element_type=jnp.float32
    )
    time_field = time_field.reshape(width_share, seq_total).astype(jnp.bfloat16)
    time_field, normed_moved = lax.optimization_barrier((time_field, normed_moved))
    spec_normed = local_freq(normed_moved)
    grad_real = (
        spec_normed[:, :, 0] * spec_gated[:, :, 0] + spec_normed[:, :, 1] * spec_gated[:, :, 1]
    )
    grad_imag = (
        spec_normed[:, :, 0] * spec_gated[:, :, 1] - spec_normed[:, :, 1] * spec_gated[:, :, 0]
    )
    spec_grad = jnp.stack([grad_real, grad_imag], axis=2).astype(jnp.bfloat16)
    partial = jnp.einsum(
        "ckrb,bj->ckrj", spec_grad.astype(jnp.float32), inner_tab,
        precision=lax.Precision.HIGHEST, preferred_element_type=jnp.float32,
    )
    coef_local = jnp.sum(
        partial[..., :FEAT] * block_cos[None, :, None, :]
        - partial[..., FEAT:] * block_sin[None, :, None, :],
        axis=1,
    ).transpose(2, 1, 0)
    home_field = lax.all_to_all(time_field, "seq", split_axis=1, concat_axis=0, tiled=True)
    coef_local, home_field = lax.optimization_barrier((coef_local, home_field))
    coef_sum = lax.all_to_all(coef_local, "seq", split_axis=0, concat_axis=2, tiled=True)
    filter_grad = coef_sum / math.sqrt(seq_total)
    conv_grad = home_field.T.astype(jnp.float32)
    normed_grad = conv_grad + skip_weight[None, :] * gated.astype(jnp.float32)
    scaled_grad = gain[None, :] * normed_grad
    row_dot = taken_together(jnp.sum(scaled_grad * upcast, axis=1), "ch")
    hidden_grad = (
        inverse_rms[:, None] * scaled_grad - upcast * (inverse_rms**3 * row_dot / D)[:, None]
    )
    return (hidden_grad.astype(jnp.bfloat16), filter_grad)


def solution(mesh):
    in_specs = (P("seq", "ch"), P("seq", "ch"), P("ch"), P("ch"), P(None, None, "ch"), P())
    out_specs = (P("seq", "ch"), P("seq", None, "ch"))
    return jax.shard_map(
        per_device, mesh=mesh, in_specs=in_specs, out_specs=out_specs, check_vma=False
    )
```

```python
import math

import jax
import jax.numpy as jnp
from jax import lax
from jax.sharding import PartitionSpec as P

D = 2048
BLOCK = 512
FEAT = 64


epsilon = 1e-06


def from_everyone(value, axis):
    copies = jnp.broadcast_to(value, (lax.axis_size(axis), *value.shape))
    return lax.all_to_all(copies, axis, split_axis=0, concat_axis=0, tiled=True)


def taken_together(value, axis):
    count = lax.axis_size(axis)
    step = 1
    while step < count:
        pairs = [(i, i ^ step) for i in range(count)]
        value = value + lax.ppermute(value, axis, pairs)
        step *= 2
    return value


def twin_table(count, sign):
    low = 64 if count % 64 == 0 else count
    indices = jnp.arange(count, dtype=jnp.int32)
    low_ids = jnp.arange(low, dtype=jnp.int32)
    high_ids = jnp.arange(count // low, dtype=jnp.int32) * low
    low_ang = 2.0 * math.pi / count * (indices[:, None] * low_ids[None, :] % count).astype(jnp.float32)
    high_ang = 2.0 * math.pi / count * (indices[:, None] * high_ids[None, :] % count).astype(jnp.float32)
    low_cos, low_sin = jnp.cos(low_ang)[:, None, :], jnp.sin(low_ang)[:, None, :]
    high_cos, high_sin = jnp.cos(high_ang)[:, :, None], jnp.sin(high_ang)[:, :, None]
    cosine = (low_cos * high_cos - low_sin * high_sin).reshape(count, count)
    sine = (low_sin * high_cos + low_cos * high_sin).reshape(count, count)
    factor = 1.0 / math.sqrt(count)
    return (cosine * factor, sign * sine * factor)


def block_matrix(count, sign):
    cosine, sine_part = twin_table(count, sign)
    half = jnp.arange(2, dtype=jnp.int32)
    same = (half[:, None, None, None] == half[None, None, :, None])
    upper = half[:, None, None, None] == 0
    sine_signed = jnp.where(upper, sine_part[None, :, None, :], -sine_part[None, :, None, :])
    return jnp.where(same, cosine[None, :, None, :], sine_signed)


def twist_leading(parts, freq_index, pos_index, seq_total, sign):
    product = (freq_index[:, None] * pos_index[None, :]).astype(jnp.float32)
    angles = 2.0 * math.pi / seq_total * product
    cosine = jnp.cos(angles)[None, :, :]
    sine_part = (sign * jnp.sin(angles))[None, :, :]
    real_part = parts[:, :, 0] * cosine - parts[:, :, 1] * sine_part
    imag_part = parts[:, :, 0] * sine_part + parts[:, :, 1] * cosine
    return jnp.stack([real_part, imag_part], axis=2)


def features(freq_index, seq_total):
    orders = 2 * jnp.arange(FEAT, dtype=jnp.int32) + 1
    product = freq_index[..., None] * orders % seq_total
    return jnp.cos(2.0 * math.pi / seq_total * product.astype(jnp.float32))


def feature_factors(inner, nblocks, seq_total):
    orders = 2 * jnp.arange(FEAT, dtype=jnp.int32) + 1
    inner_ids = jnp.arange(inner, dtype=jnp.int32)
    block_ids = jnp.arange(nblocks, dtype=jnp.int32)
    inner_prod = (inner_ids[:, None] * orders[None, :]) % inner
    block_prod = (block_ids[:, None] * orders[None, :]) % seq_total
    inner_ang = 2.0 * math.pi / inner * inner_prod.astype(jnp.float32)
    block_ang = 2.0 * math.pi / seq_total * block_prod.astype(jnp.float32)
    inner_tab = jnp.concatenate([jnp.cos(inner_ang), jnp.sin(inner_ang)], axis=1)
    return inner_tab, jnp.cos(block_ang), jnp.sin(block_ang)


def per_device(hidden_in, grad_out, norm_gain, skip_weight, filter_coef, run_lengths):
    local_tokens = hidden_in.shape[0]
    local_width = hidden_in.shape[1]
    seq_parts = lax.axis_size("seq")
    seq_rank = lax.axis_index("seq")
    seq_total = local_tokens * seq_parts
    nblocks = seq_total // BLOCK
    upcast = hidden_in.astype(jnp.float32)
    square_sums = taken_together(jnp.sum(upcast * upcast, axis=1), "ch")
    inverse_rms = lax.rsqrt(square_sums / D + epsilon)
    gain = norm_gain.astype(jnp.float32)
    normed = (upcast * inverse_rms[:, None] * gain[None, :]).astype(jnp.bfloat16)
    run_ends = jnp.cumsum(run_lengths)
    positions = seq_rank * local_tokens + jnp.arange(local_tokens, dtype=jnp.int32)
    run_index = jnp.sum((run_ends[None, :] <= positions[:, None]).astype(jnp.int32), axis=1)
    keep = run_index % 2 == 0
    gated = jnp.where(keep[:, None], grad_out, jnp.zeros_like(grad_out))
    forward_first = jnp.stack(twin_table(nblocks, -1.0), axis=2).astype(jnp.bfloat16)
    forward_second = block_matrix(BLOCK, -1.0).astype(jnp.bfloat16)
    back_first = block_matrix(BLOCK, 1.0).astype(jnp.bfloat16)
    cosine, sine_part = twin_table(nblocks, 1.0)
    back_second = jnp.stack([cosine, -sine_part], axis=1).astype(jnp.bfloat16)
    block_ids = jnp.arange(nblocks, dtype=jnp.int32)
    all_inner = jnp.arange(BLOCK, dtype=jnp.int32)
    width_share = local_width // seq_parts
    gated, inverse_rms = lax.optimization_barrier((gated, inverse_rms))
    gated_moved = lax.all_to_all(gated.T, "seq", split_axis=0, concat_axis=1, tiled=True)
    gated_moved, normed = lax.optimization_barrier((gated_moved, normed))
    normed_moved = lax.all_to_all(normed.T, "seq", split_axis=0, concat_axis=1, tiled=True)
    moved = (normed_moved, gated_moved)
    coef_part = lax.dynamic_slice_in_dim(filter_coef, seq_rank * width_share, width_share, 2)

    def local_freq(field):
        blocks = field.reshape(width_share, nblocks, BLOCK)
        parts = jnp.einsum(
            "cnm,nkr->ckrm", blocks, forward_first, preferred_element_type=jnp.float32
        )
        turned = twist_leading(parts, block_ids, all_inner, seq_total, -1.0).astype(jnp.bfloat16)
        return jnp.einsum(
            "ckrm,rmsj->cksj", turned, forward_second, preferred_element_type=jnp.float32
        )

    spec_gated = local_freq(moved[1])
    inner_tab, block_cos, block_sin = feature_factors(BLOCK, nblocks, seq_total)
    coef_t = coef_part.astype(jnp.float32).transpose(2, 1, 0)[:, None, :, :]
    coef_mix = jnp.concatenate(
        [block_cos[None, :, None, :] * coef_t, -block_sin[None, :, None, :] * coef_t], axis=3
    )
    response = jnp.einsum(
        "ckrj,bj->ckrb", coef_mix, inner_tab,
        precision=lax.Precision.HIGHEST, preferred_element_type=jnp.float32,
    )
    prod_real = response[:, :, 0] * spec_gated[:, :, 0] + response[:, :, 1] * spec_gated[:, :, 1]
    prod_imag = response[:, :, 0] * spec_gated[:, :, 1] - response[:, :, 1] * spec_gated[:, :, 0]
    product = jnp.stack([prod_real, prod_imag], axis=2).astype(jnp.bfloat16)
    back_parts = jnp.einsum(
        "ckrm,rmsj->cksj", product, back_first, preferred_element_type=jnp.float32
    )
    back_twisted = twist_leading(back_parts, block_ids, all_inner, seq_total, 1.0).astype(
        jnp.bfloat16
    )
    time_field = jnp.einsum(
        "ckrm,krn->cnm", back_twisted, back_second, preferred_element_type=jnp.float32
    )
    time_field = time_field.reshape(width_share, seq_total).astype(jnp.bfloat16)
    time_field, normed_moved = lax.optimization_barrier((time_field, normed_moved))
    spec_normed = local_freq(normed_moved)
    grad_real = (
        spec_normed[:, :, 0] * spec_gated[:, :, 0] + spec_normed[:, :, 1] * spec_gated[:, :, 1]
    )
    grad_imag = (
        spec_normed[:, :, 0] * spec_gated[:, :, 1] - spec_normed[:, :, 1] * spec_gated[:, :, 0]
    )
    spec_grad = jnp.stack([grad_real, grad_imag], axis=2).astype(jnp.bfloat16)
    partial = jnp.einsum(
        "ckrb,bj->ckrj", spec_grad.astype(jnp.float32), inner_tab,
        precision=lax.Precision.HIGHEST, preferred_element_type=jnp.float32,
    )
    coef_local = jnp.sum(
        partial[..., :FEAT] * block_cos[None, :, None, :]
        - partial[..., FEAT:] * block_sin[None, :, None, :],
        axis=1,
    ).transpose(2, 1, 0)
    coef_rows = FEAT // seq_parts
    coef_blocks = coef_local.reshape(seq_parts, coef_rows * 2, width_share).transpose(2, 0, 1)
    coef_high = coef_blocks.astype(jnp.bfloat16)
    coef_low = (coef_blocks - coef_high.astype(jnp.float32)).astype(jnp.bfloat16)
    outgoing = jnp.concatenate(
        [time_field.reshape(width_share, seq_parts, local_tokens), coef_high, coef_low], axis=2
    )
    incoming = lax.all_to_all(outgoing, "seq", split_axis=1, concat_axis=0, tiled=True)
    home_field = incoming[:, 0, :local_tokens]
    coef_parts = incoming[:, 0, local_tokens:].astype(jnp.float32).reshape(local_width, 2, coef_rows, 2)
    coef_sum = (coef_parts[:, 0] + coef_parts[:, 1]).transpose(1, 2, 0)
    filter_grad = coef_sum / math.sqrt(seq_total)
    conv_grad = home_field.T.astype(jnp.float32)
    normed_grad = conv_grad + skip_weight[None, :] * gated.astype(jnp.float32)
    scaled_grad = gain[None, :] * normed_grad
    row_dot = taken_together(jnp.sum(scaled_grad * upcast, axis=1), "ch")
    hidden_grad = (
        inverse_rms[:, None] * scaled_grad - upcast * (inverse_rms**3 * row_dot / D)[:, None]
    )
    return (hidden_grad.astype(jnp.bfloat16), filter_grad)


def solution(mesh):
    in_specs = (P("seq", "ch"), P("seq", "ch"), P("ch"), P("ch"), P(None, None, "ch"), P())
    out_specs = (P("seq", "ch"), P("seq", None, "ch"))
    return jax.shard_map(
        per_device, mesh=mesh, in_specs=in_specs, out_specs=out_specs, check_vma=False
    )
```
